32 devices in a mesh: seq: 8 (over y, x, core), fsdp: 4 (over z).
Axes of the slice: x: 2, y: 2, z: 4, core: 2. Of those that a mesh axis runs over, the one named last changes fastest.
Arguments:
- query_states: bfloat16 [2048, 4096], P('seq', 'fsdp'), may hold values from -24 to 24
- key_states: bfloat16 [2048, 4096], P('seq', 'fsdp'), may hold values from -6 to 6
- value_states: bfloat16 [2048, 4096], P('seq', 'fsdp'), may hold values from -6 to 6
- positions: int32 [2048], P('seq'), may hold values from 0 to 2047, as said below
- out_weight: bfloat16 [4096, 5120], P('fsdp', 'seq'), may hold values from -1 to 1
- cotangent: bfloat16 [2048, 5120], P('seq', 'fsdp'), may hold values from -0.59765625 to 0.59765625
Outputs:
- attn_output: float32 [2048, 5120], P('seq', 'fsdp')
- grad_queries: float32 [2048, 4096], P('seq', 'fsdp')
- grad_keys: float32 [2048, 4096], P('seq', 'fsdp')
- grad_values: float32 [2048, 4096], P('seq', 'fsdp')
- grad_weight: float32 [4096, 5120], P('fsdp', 'seq')
The draws below stay inside these ranges and needn't reach their ends.
Inputs may be any that keep to these rules, and one draw needn't show every extreme that they name: A permutation of 0 to 2047; each aligned block of 256 rows holds, in increasing order, the positions of one residue class modulo 2048 // 256.
All inputs are finite; a program needn't handle non-finite values.
Results may differ from the reference program's by a relative error of at most 0.02.
Values may be sent and summed in bfloat16 or wider, within the bound.
No kernel may reach another device: no remote copies, remote signals or barrier semaphores. Data moves between devices by JAX's collectives and lax.ppermute only.
A program may use at most 128 MiB of HBM per device.

```python
import jax
import jax.numpy as jnp
from jax import lax

D = 5120
HEADS = 32
HEAD_DIM = 128
TOK_DEV = 256
SEQ_LEN = 2048
N_FSDP = 4


def drawn_pair(key):
    base = jax.random.fold_in(key, 11)
    key_query, key_key = jax.random.split(base, 2)
    shape = (SEQ_LEN, HEADS, HEAD_DIM)
    query_draw = 1.2 * jax.random.truncated_normal(key_query, -5.0, 5.0, shape, jnp.float32)
    key_draw = 1.2 * jax.random.truncated_normal(key_key, -5.0, 5.0, shape, jnp.float32)
    return (query_draw.reshape(SEQ_LEN, HEADS * HEAD_DIM), key_draw.reshape(SEQ_LEN, HEADS * HEAD_DIM))


def draw_query_states(key, part):
    return drawn_pair(key)[0].astype(jnp.bfloat16)


def draw_key_states(key, part):
    return drawn_pair(key)[1].astype(jnp.bfloat16)


def draw_positions(key, part):
    blocks = SEQ_LEN // TOK_DEV
    residues = jax.random.permutation(jax.random.fold_in(key, 23), blocks).astype(jnp.int32)
    row_index = jnp.arange(SEQ_LEN, dtype=jnp.int32)
    block_index = row_index // TOK_DEV
    local_row = row_index % TOK_DEV
    return (local_row * blocks + residues[block_index]).astype(jnp.int32)


def raised(values, key, source, target, parts, factor):
    owner, partner = [(jnp.arange(values.shape[position]) // (values.shape[position] // parts)).reshape([-1 if axis == position else 1 for axis in range(values.ndim)]) for position in (source, target)]
    chosen = jax.random.permutation(key, parts)[partner]
    strong = (owner == chosen) | (owner == (partner + parts // 2) % parts)
    return jnp.where(strong, factor * values, values)


def levels(own_key, extent, pieces, smallest, high):
    factor_of, own = 1.0, jax.random.fold_in(own_key, 6)
    for axis_at, parts in pieces:
        steps = jnp.exp(jax.random.uniform(jax.random.fold_in(own, axis_at), (parts,), jnp.float32, smallest / len(pieces), high / len(pieces)))
        factor_of = factor_of * jnp.repeat(steps, extent[axis_at] // parts).reshape([-1 if axis == axis_at else 1 for axis in range(len(extent))])
    return factor_of


def noise(own_key, dims, spread, reach, cuts=(), kind=jnp.bfloat16):
    drawn = jax.random.normal(own_key, dims, jnp.float32) * spread
    if len(cuts) > 0:
        drawn = levels(own_key, dims, cuts, -0.22, 0.18) * drawn
    return jnp.clip(drawn, min=-reach, max=reach).astype(kind)


def bell_draw_with(own_key, extent, deviation, reach, shards, heavy, kind=jnp.bfloat16):
    entries = deviation * jax.random.normal(own_key, extent, jnp.float32)
    if shards:
        entries = entries * levels(own_key, extent, shards, -0.22, 0.18)
    return jnp.clip(raised(entries, jax.random.fold_in(own_key, 3), *heavy), -reach, reach).astype(kind)


def setup_inputs(seed: int = 0) -> dict:
    keys = jax.random.split(jax.random.key(seed), 7)
    return {
        "query_states": draw_query_states(jax.random.fold_in(keys[6], 71), 0),
        "key_states": draw_key_states(jax.random.fold_in(keys[6], 71), 0),
        "value_states": noise(keys[2], (SEQ_LEN, HEADS * HEAD_DIM), 1.0, 6.0, ((0, 8), (1, 4))),
        "positions": draw_positions(jax.random.fold_in(keys[6], 71), 0),
        "out_weight": bell_draw_with(keys[4], (HEADS * HEAD_DIM, D), (HEADS * HEAD_DIM // 64) ** -0.5, 1.0, ((0, 4), (1, 8)), (0, 1, 8, 2.0)),
        "cotangent": bell_draw_with(keys[5], (SEQ_LEN, D), 0.1, 0.59765625, ((0, 8), (1, 4)), (0, 1, 8, 2.0)),
    }


blocked = -1e30


def split_heads(matrix):
    return matrix.reshape(matrix.shape[0], HEADS, HEAD_DIM).transpose(1, 0, 2)


def join_heads(stacked):
    return stacked.transpose(1, 0, 2).reshape(stacked.shape[1], HEADS * HEAD_DIM)


def reference(query_states, key_states, value_states, positions, out_weight, cotangent):
    score_scale = HEAD_DIM ** -0.5
    visible = positions[None, :] <= positions[:, None]

    def head_scores(query_rows, key_rows):
        raw = jnp.dot(query_rows, key_rows.T, preferred_element_type=jnp.float32) * score_scale
        return jnp.where(visible, raw, blocked)

    def forward_head(operands):
        query_rows, key_rows, value_rows = operands
        scores = head_scores(query_rows, key_rows)
        row_max = jnp.max(scores, axis=1)
        log_total = row_max + jnp.log(jnp.sum(jnp.exp(scores - row_max[:, None]), axis=1))
        weights = jnp.exp(scores - log_total[:, None]).astype(jnp.bfloat16)
        output_rows = jnp.dot(weights, value_rows, preferred_element_type=jnp.float32).astype(jnp.bfloat16)
        return log_total, output_rows

    query_heads = split_heads(query_states)
    key_heads = split_heads(key_states)
    value_heads = split_heads(value_states)
    log_totals, attended_heads = lax.map(forward_head, (query_heads, key_heads, value_heads))
    attended = join_heads(attended_heads)

    group_width = (HEADS // N_FSDP) * HEAD_DIM

    def add_group(running, group_index):
        columns = lax.dynamic_slice_in_dim(attended, group_index * group_width, group_width, 1)
        weight_rows = lax.dynamic_slice_in_dim(out_weight, group_index * group_width, group_width, 0)
        partial_sum = jnp.dot(columns, weight_rows, preferred_element_type=jnp.float32).astype(jnp.bfloat16)
        partial_sum = lax.optimization_barrier(partial_sum)
        return running + partial_sum.astype(jnp.float32), None

    summed, _ = lax.scan(add_group, jnp.zeros((SEQ_LEN, D), jnp.float32), jnp.arange(N_FSDP, dtype=jnp.int32))
    attn_output = summed

    grad_attended = jnp.dot(cotangent, out_weight.T, preferred_element_type=jnp.float32).astype(jnp.bfloat16)
    grad_weight = jnp.dot(attended.T, cotangent, preferred_element_type=jnp.float32)

    def backward_head(operands):
        query_rows, key_rows, value_rows, grad_rows, output_rows, log_total = operands
        row_delta = jnp.sum(grad_rows.astype(jnp.float32) * output_rows.astype(jnp.float32), axis=1)
        scores = head_scores(query_rows, key_rows)
        probs = jnp.exp(scores - log_total[:, None])
        grad_probs = jnp.dot(grad_rows, value_rows.T, preferred_element_type=jnp.float32)
        grad_scores = (probs * (grad_probs - row_delta[:, None])).astype(jnp.bfloat16)
        grad_query = jnp.dot(grad_scores, key_rows, preferred_element_type=jnp.float32) * score_scale
        grad_key = jnp.dot(grad_scores.T, query_rows, preferred_element_type=jnp.float32) * score_scale
        grad_value = jnp.dot(probs.astype(jnp.bfloat16).T, grad_rows, preferred_element_type=jnp.float32)
        return grad_query, grad_key, grad_value

    grads = lax.map(backward_head, (query_heads, key_heads, value_heads, split_heads(grad_attended), attended_heads, log_totals))
    return attn_output, join_heads(grads[0]), join_heads(grads[1]), join_heads(grads[2]), grad_weight
```

```python
import jax
import jax.numpy as jnp
from jax import lax
from jax.sharding import PartitionSpec as P

HEAD_DIM = 128


blocked = -1e30


def split_heads(matrix):
    return matrix.reshape(matrix.shape[0], -1, HEAD_DIM)


def masked_scores(query_rows, key_rows, query_pos, key_pos):
    raw = jnp.einsum(
        "qhd,khd->hqk", query_rows, key_rows, preferred_element_type=jnp.float32
    ) * HEAD_DIM ** (-0.5)
    visible = key_pos[None, None, :] <= query_pos[None, :, None]
    return jnp.where(visible, raw, blocked)


def shards(query_states, key_states, value_states, positions, out_weight, cotangent):
    local_tokens = query_states.shape[0]
    query_heads = split_heads(query_states)
    local_heads = query_heads.shape[1]
    all_keys = lax.all_gather(key_states, "seq", axis=0, tiled=True)
    all_values = lax.all_gather(value_states, "seq", axis=0, tiled=True)
    all_pos = lax.all_gather(positions, "seq", axis=0, tiled=True)
    key_heads = split_heads(all_keys)
    value_heads = split_heads(all_values)
    scores = masked_scores(query_heads, key_heads, positions, all_pos)
    row_max = jnp.max(scores, axis=2)
    log_total = row_max + jnp.log(jnp.sum(jnp.exp(scores - row_max[:, :, None]), axis=2))
    probs = jnp.exp(scores - log_total[:, :, None])
    weights = probs.astype(jnp.bfloat16)
    attended = jnp.einsum(
        "hqk,khd->qhd", weights, value_heads, preferred_element_type=jnp.float32
    )
    attended_heads = attended.astype(jnp.bfloat16)
    attended_flat = attended_heads.reshape(local_tokens, local_heads * HEAD_DIM)
    weight_full = lax.all_gather(out_weight, "seq", axis=1, tiled=True)
    partial_sum = jnp.dot(attended_flat, weight_full, preferred_element_type=jnp.float32).astype(
        jnp.bfloat16
    )
    attn_output = lax.psum_scatter(partial_sum, "fsdp", scatter_dimension=1, tiled=True).astype(
        jnp.float32
    )
    cotangent_full = lax.all_gather(cotangent, "fsdp", axis=1, tiled=True)
    grad_attended = jnp.einsum(
        "td,hd->th", cotangent_full, weight_full, preferred_element_type=jnp.float32
    ).astype(jnp.bfloat16)
    all_attended = lax.all_gather(attended_flat, "seq", axis=0, tiled=True)
    cotangent_cols = lax.all_to_all(cotangent_full, "seq", 1, 0, tiled=True)
    grad_weight = jnp.einsum(
        "th,td->hd", all_attended, cotangent_cols, preferred_element_type=jnp.float32
    )
    grad_heads = split_heads(grad_attended)
    row_delta = jnp.sum(
        grad_heads.astype(jnp.float32) * attended_heads.astype(jnp.float32), axis=2
    ).T
    grad_probs = jnp.einsum(
        "qhd,khd->hqk", grad_heads, value_heads, preferred_element_type=jnp.float32
    )
    grad_scores = (probs * (grad_probs - row_delta[:, :, None])).astype(jnp.bfloat16)
    query_sum = jnp.einsum(
        "hqk,khd->qhd", grad_scores, key_heads, preferred_element_type=jnp.float32
    )
    key_part = jnp.einsum(
        "hqk,qhd->khd", grad_scores, query_heads, preferred_element_type=jnp.float32
    )
    value_part = jnp.einsum(
        "hqk,qhd->khd", weights, grad_heads, preferred_element_type=jnp.float32
    )
    key_sum = lax.psum_scatter(key_part, "seq", scatter_dimension=0, tiled=True)
    value_sum = lax.psum_scatter(value_part, "seq", scatter_dimension=0, tiled=True)
    score_scale = HEAD_DIM ** (-0.5)
    grad_queries = (query_sum * score_scale).reshape(local_tokens, local_heads * HEAD_DIM)
    grad_keys = (key_sum * score_scale).reshape(local_tokens, local_heads * HEAD_DIM)
    grad_values = value_sum.reshape(local_tokens, local_heads * HEAD_DIM)
    return (attn_output, grad_queries, grad_keys, grad_values, grad_weight)


def solution(mesh):
    in_specs = (
        P("seq", "fsdp"),
        P("seq", "fsdp"),
        P("seq", "fsdp"),
        P("seq"),
        P("fsdp", "seq"),
        P("seq", "fsdp"),
    )
    out_specs = (
        P("seq", "fsdp"),
        P("seq", "fsdp"),
        P("seq", "fsdp"),
        P("seq", "fsdp"),
        P("fsdp", "seq"),
    )
    return jax.shard_map(shards, mesh=mesh, in_specs=in_specs, out_specs=out_specs, check_vma=False)
```

```python
import jax
import jax.numpy as jnp
from jax import lax
from jax.sharding import PartitionSpec as P

HEAD_DIM = 128


blocked = -1e30


def split_heads(matrix):
    return matrix.reshape(matrix.shape[0], -1, HEAD_DIM)


def masked_scores(query_rows, key_rows, query_pos, key_pos):
    raw = jnp.einsum(
        "qhd,khd->hqk", query_rows, key_rows, preferred_element_type=jnp.float32
    ) * HEAD_DIM ** (-0.5)
    visible = key_pos[None, None, :] <= query_pos[None, :, None]
    return jnp.where(visible, raw, blocked)


def shards(query_states, key_states, value_states, positions, out_weight, cotangent):
    local_tokens = query_states.shape[0]
    query_heads = split_heads(query_states)
    local_heads = query_heads.shape[1]
    all_keys = lax.all_gather(key_states, "seq", axis=0, tiled=True)
    all_values = lax.all_gather(value_states, "seq", axis=0, tiled=True)
    all_pos = lax.all_gather(positions, "seq", axis=0, tiled=True)
    key_heads = split_heads(all_keys)
    value_heads = split_heads(all_values)
    scores = masked_scores(query_heads, key_heads, positions, all_pos)
    row_max = jnp.max(scores, axis=2)
    log_total = row_max + jnp.log(jnp.sum(jnp.exp(scores - row_max[:, :, None]), axis=2))
    probs = jnp.exp(scores - log_total[:, :, None])
    weights = probs.astype(jnp.bfloat16)
    attended = jnp.einsum(
        "hqk,khd->qhd", weights, value_heads, preferred_element_type=jnp.float32
    )
    attended_heads = attended.astype(jnp.bfloat16)
    attended_flat = attended_heads.reshape(local_tokens, local_heads * HEAD_DIM)
    weight_full = lax.all_gather(out_weight, "seq", axis=1, tiled=True)
    partial_sum = jnp.dot(attended_flat, weight_full, preferred_element_type=jnp.float32).astype(
        jnp.bfloat16
    )
    attn_output = lax.psum_scatter(partial_sum, "fsdp", scatter_dimension=1, tiled=True).astype(
        jnp.float32
    )
    cotangent_full = lax.all_gather(cotangent, "fsdp", axis=1, tiled=True)
    grad_attended = jnp.einsum(
        "td,hd->th", cotangent_full, weight_full, preferred_element_type=jnp.float32
    ).astype(jnp.bfloat16)
    all_attended = lax.all_gather(attended_flat, "seq", axis=0, tiled=True)
    cotangent_cols = lax.all_to_all(cotangent_full, "seq", 1, 0, tiled=True)
    grad_weight = jnp.einsum(
        "th,td->hd", all_attended, cotangent_cols, preferred_element_type=jnp.float32
    )
    grad_heads = split_heads(grad_attended)
    row_delta = jnp.sum(
        grad_heads.astype(jnp.float32) * attended_heads.astype(jnp.float32), axis=2
    ).T
    grad_probs = jnp.einsum(
        "qhd,khd->hqk", grad_heads, value_heads, preferred_element_type=jnp.float32
    )
    grad_scores = (probs * (grad_probs - row_delta[:, :, None])).astype(jnp.bfloat16)
    query_sum = jnp.einsum(
        "hqk,khd->qhd", grad_scores, key_heads, preferred_element_type=jnp.float32
    )
    key_part = jnp.einsum(
        "hqk,qhd->khd", grad_scores, query_heads, preferred_element_type=jnp.float32
    )
    value_part = jnp.einsum(
        "hqk,qhd->khd", weights, grad_heads, preferred_element_type=jnp.float32
    )
    both_parts = jnp.concatenate([key_part, value_part], axis=1).astype(jnp.bfloat16)
    both_sums = lax.psum_scatter(both_parts, "seq", scatter_dimension=0, tiled=True).astype(
        jnp.float32
    )
    key_sum = both_sums[:, :local_heads]
    value_sum = both_sums[:, local_heads:]
    score_scale = HEAD_DIM ** (-0.5)
    grad_queries = (query_sum * score_scale).reshape(local_tokens, local_heads * HEAD_DIM)
    grad_keys = (key_sum * score_scale).reshape(local_tokens, local_heads * HEAD_DIM)
    grad_values = value_sum.reshape(local_tokens, local_heads * HEAD_DIM)
    return (attn_output, grad_queries, grad_keys, grad_values, grad_weight)


def solution(mesh):
    in_specs = (
        P("seq", "fsdp"),
        P("seq", "fsdp"),
        P("seq", "fsdp"),
        P("seq"),
        P("fsdp", "seq"),
        P("seq", "fsdp"),
    )
    out_specs = (
        P("seq", "fsdp"),
        P("seq", "fsdp"),
        P("seq", "fsdp"),
        P("seq", "fsdp"),
        P("fsdp", "seq"),
    )
    return jax.shard_map(shards, mesh=mesh, in_specs=in_specs, out_specs=out_specs, check_vma=False)
```

```python
import jax
import jax.numpy as jnp
from jax import lax
from jax.sharding import PartitionSpec as P

HEAD_DIM = 128


blocked = -1e30


def split_heads(matrix):
    return matrix.reshape(matrix.shape[0], -1, HEAD_DIM)


def masked_scores(query_rows, key_rows, query_pos, key_pos):
    raw = jnp.einsum(
        "qhd,khd->hqk", query_rows, key_rows, preferred_element_type=jnp.float32
    ) * HEAD_DIM ** (-0.5)
    visible = key_pos[None, None, :] <= query_pos[None, :, None]
    return jnp.where(visible, raw, blocked)


def shift_pieces(block, axis):
    count = lax.axis_size(axis)
    pieces = [block]
    for distance in range(1, count):
        route = [(i, (i + distance) % count) for i in range(count)]
        pieces.append(lax.ppermute(block, axis, route))
    return pieces


def permute_gather(block, axis, dim):
    count = lax.axis_size(axis)
    me = lax.axis_index(axis)
    width = block.shape[dim]
    shape = list(block.shape)
    shape[dim] = width * count
    full = jnp.zeros(shape, block.dtype)
    for distance, piece in enumerate(shift_pieces(block, axis)):
        start = [0] * block.ndim
        start[dim] = ((me - distance) % count) * width
        full = lax.dynamic_update_slice(full, piece, start)
    return full


def permute_sum_scatter(block, axis, dim):
    count = lax.axis_size(axis)
    me = lax.axis_index(axis)
    width = block.shape[dim] // count
    total = lax.dynamic_slice_in_dim(block, me * width, width, dim).astype(jnp.float32)
    for distance in range(1, count):
        route = [(i, (i + distance) % count) for i in range(count)]
        piece = lax.dynamic_slice_in_dim(block, ((me + distance) % count) * width, width, dim)
        total = total + lax.ppermute(piece, axis, route).astype(jnp.float32)
    return total


def shards(query_states, key_states, value_states, positions, out_weight, cotangent):
    local_tokens = query_states.shape[0]
    query_heads = split_heads(query_states)
    local_heads = query_heads.shape[1]
    all_keys = lax.all_gather(key_states, "seq", axis=0, tiled=True)
    all_values = lax.all_gather(value_states, "seq", axis=0, tiled=True)
    all_pos = lax.all_gather(positions, "seq", axis=0, tiled=True)
    key_heads = split_heads(all_keys)
    value_heads = split_heads(all_values)
    scores = masked_scores(query_heads, key_heads, positions, all_pos)
    row_max = jnp.max(scores, axis=2)
    log_total = row_max + jnp.log(jnp.sum(jnp.exp(scores - row_max[:, :, None]), axis=2))
    probs = jnp.exp(scores - log_total[:, :, None])
    weights = probs.astype(jnp.bfloat16)
    attended = jnp.einsum(
        "hqk,khd->qhd", weights, value_heads, preferred_element_type=jnp.float32
    )
    attended_heads = attended.astype(jnp.bfloat16)
    attended_flat = attended_heads.reshape(local_tokens, local_heads * HEAD_DIM)
    weight_full = lax.all_gather(out_weight, "seq", axis=1, tiled=True)
    partial_sum = jnp.dot(attended_flat, weight_full, preferred_element_type=jnp.float32).astype(
        jnp.bfloat16
    )
    attn_output = permute_sum_scatter(partial_sum, "fsdp", 1)
    cotangent_full = permute_gather(cotangent, "fsdp", 1)
    grad_attended = jnp.einsum(
        "td,hd->th", cotangent_full, weight_full, preferred_element_type=jnp.float32
    ).astype(jnp.bfloat16)
    all_attended = lax.all_gather(attended_flat, "seq", axis=0, tiled=True)
    cotangent_cols = lax.all_to_all(cotangent_full, "seq", 1, 0, tiled=True)
    grad_weight = jnp.einsum(
        "th,td->hd", all_attended, cotangent_cols, preferred_element_type=jnp.float32
    )
    grad_heads = split_heads(grad_attended)
    row_delta = jnp.sum(
        grad_heads.astype(jnp.float32) * attended_heads.astype(jnp.float32), axis=2
    ).T
    grad_probs = jnp.einsum(
        "qhd,khd->hqk", grad_heads, value_heads, preferred_element_type=jnp.float32
    )
    grad_scores = (probs * (grad_probs - row_delta[:, :, None])).astype(jnp.bfloat16)
    query_sum = jnp.einsum(
        "hqk,khd->qhd", grad_scores, key_heads, preferred_element_type=jnp.float32
    )
    key_part = jnp.einsum(
        "hqk,qhd->khd", grad_scores, query_heads, preferred_element_type=jnp.float32
    )
    value_part = jnp.einsum(
        "hqk,qhd->khd", weights, grad_heads, preferred_element_type=jnp.float32
    )
    both_parts = jnp.concatenate([key_part, value_part], axis=1).astype(jnp.bfloat16)
    both_sums = lax.psum_scatter(both_parts, "seq", scatter_dimension=0, tiled=True).astype(
        jnp.float32
    )
    key_sum = both_sums[:, :local_heads]
    value_sum = both_sums[:, local_heads:]
    score_scale = HEAD_DIM ** (-0.5)
    grad_queries = (query_sum * score_scale).reshape(local_tokens, local_heads * HEAD_DIM)
    grad_keys = (key_sum * score_scale).reshape(local_tokens, local_heads * HEAD_DIM)
    grad_values = value_sum.reshape(local_tokens, local_heads * HEAD_DIM)
    return (attn_output, grad_queries, grad_keys, grad_values, grad_weight)


def solution(mesh):
    in_specs = (
        P("seq", "fsdp"),
        P("seq", "fsdp"),
        P("seq", "fsdp"),
        P("seq"),
        P("fsdp", "seq"),
        P("seq", "fsdp"),
    )
    out_specs = (
        P("seq", "fsdp"),
        P("seq", "fsdp"),
        P("seq", "fsdp"),
        P("seq", "fsdp"),
        P("fsdp", "seq"),
    )
    return jax.shard_map(shards, mesh=mesh, in_specs=in_specs, out_specs=out_specs, check_vma=False)
```

```python
import jax
import jax.numpy as jnp
from jax import lax
from jax.sharding import PartitionSpec as P

HEAD_DIM = 128


blocked = -1e30


def split_heads(matrix):
    return matrix.reshape(matrix.shape[0], -1, HEAD_DIM)


def masked_scores(query_rows, key_rows, query_pos, key_pos):
    raw = jnp.einsum(
        "qhd,khd->hqk", query_rows, key_rows, preferred_element_type=jnp.float32
    ) * HEAD_DIM ** (-0.5)
    visible = key_pos[None, None, :] <= query_pos[None, :, None]
    return jnp.where(visible, raw, blocked)


def shift_pieces(block, axis):
    count = lax.axis_size(axis)
    pieces = [block]
    for distance in range(1, count):
        route = [(i, (i + distance) % count) for i in range(count)]
        pieces.append(lax.ppermute(block, axis, route))
    return pieces


def permute_gather(block, axis, dim):
    count = lax.axis_size(axis)
    me = lax.axis_index(axis)
    width = block.shape[dim]
    shape = list(block.shape)
    shape[dim] = width * count
    full = jnp.zeros(shape, block.dtype)
    for distance, piece in enumerate(shift_pieces(block, axis)):
        start = [0] * block.ndim
        start[dim] = ((me - distance) % count) * width
        full = lax.dynamic_update_slice(full, piece, start)
    return full


def pair_gather(block, axis, dim):
    count = lax.axis_size(axis)
    if count % 2:
        return permute_gather(block, axis, dim)
    me = lax.axis_index(axis)
    mate = me + 1 - 2 * (me % 2)
    chips = count // 2
    width = block.shape[dim]
    shape = list(block.shape)
    shape[dim] = width * count
    full = jnp.zeros(shape, block.dtype)
    pair_route = [(i, i ^ 1) for i in range(count)]
    for step in range(chips):
        if step:
            route = [(i, (i + 2 * step) % count) for i in range(count)]
            piece = lax.ppermute(block, axis, route)
        else:
            piece = block
        mate_piece = lax.ppermute(piece, axis, pair_route)
        for source, part in (((me - 2 * step) % count, piece), ((mate - 2 * step) % count, mate_piece)):
            start = [0] * block.ndim
            start[dim] = source * width
            full = lax.dynamic_update_slice(full, part, start)
    return full


def permute_sum_scatter(block, axis, dim):
    count = lax.axis_size(axis)
    me = lax.axis_index(axis)
    width = block.shape[dim] // count
    total = lax.dynamic_slice_in_dim(block, me * width, width, dim).astype(jnp.float32)
    for distance in range(1, count):
        route = [(i, (i + distance) % count) for i in range(count)]
        piece = lax.dynamic_slice_in_dim(block, ((me + distance) % count) * width, width, dim)
        total = total + lax.ppermute(piece, axis, route).astype(jnp.float32)
    return total


def shards(query_states, key_states, value_states, positions, out_weight, cotangent):
    local_tokens = query_states.shape[0]
    query_heads = split_heads(query_states)
    local_heads = query_heads.shape[1]
    all_keys = lax.all_gather(key_states, "seq", axis=0, tiled=True)
    all_values = lax.all_gather(value_states, "seq", axis=0, tiled=True)
    all_pos = lax.all_gather(positions, "seq", axis=0, tiled=True)
    key_heads = split_heads(all_keys)
    value_heads = split_heads(all_values)
    scores = masked_scores(query_heads, key_heads, positions, all_pos)
    row_max = jnp.max(scores, axis=2)
    log_total = row_max + jnp.log(jnp.sum(jnp.exp(scores - row_max[:, :, None]), axis=2))
    probs = jnp.exp(scores - log_total[:, :, None])
    weights = probs.astype(jnp.bfloat16)
    attended = jnp.einsum(
        "hqk,khd->qhd", weights, value_heads, preferred_element_type=jnp.float32
    )
    attended_heads = attended.astype(jnp.bfloat16)
    attended_flat = attended_heads.reshape(local_tokens, local_heads * HEAD_DIM)
    weight_full = pair_gather(out_weight, "seq", 1)
    partial_sum = jnp.dot(attended_flat, weight_full, preferred_element_type=jnp.float32).astype(
        jnp.bfloat16
    )
    attn_output = permute_sum_scatter(partial_sum, "fsdp", 1)
    cotangent_full = permute_gather(cotangent, "fsdp", 1)
    grad_attended = jnp.einsum(
        "td,hd->th", cotangent_full, weight_full, preferred_element_type=jnp.float32
    ).astype(jnp.bfloat16)
    all_attended = lax.all_gather(attended_flat, "seq", axis=0, tiled=True)
    cotangent_cols = lax.all_to_all(cotangent_full, "seq", 1, 0, tiled=True)
    grad_weight = jnp.einsum(
        "th,td->hd", all_attended, cotangent_cols, preferred_element_type=jnp.float32
    )
    grad_heads = split_heads(grad_attended)
    row_delta = jnp.sum(
        grad_heads.astype(jnp.float32) * attended_heads.astype(jnp.float32), axis=2
    ).T
    grad_probs = jnp.einsum(
        "qhd,khd->hqk", grad_heads, value_heads, preferred_element_type=jnp.float32
    )
    grad_scores = (probs * (grad_probs - row_delta[:, :, None])).astype(jnp.bfloat16)
    query_sum = jnp.einsum(
        "hqk,khd->qhd", grad_scores, key_heads, preferred_element_type=jnp.float32
    )
    key_part = jnp.einsum(
        "hqk,qhd->khd", grad_scores, query_heads, preferred_element_type=jnp.float32
    )
    value_part = jnp.einsum(
        "hqk,qhd->khd", weights, grad_heads, preferred_element_type=jnp.float32
    )
    both_parts = jnp.concatenate([key_part, value_part], axis=1).astype(jnp.bfloat16)
    both_sums = lax.psum_scatter(both_parts, "seq", scatter_dimension=0, tiled=True).astype(
        jnp.float32
    )
    key_sum = both_sums[:, :local_heads]
    value_sum = both_sums[:, local_heads:]
    score_scale = HEAD_DIM ** (-0.5)
    grad_queries = (query_sum * score_scale).reshape(local_tokens, local_heads * HEAD_DIM)
    grad_keys = (key_sum * score_scale).reshape(local_tokens, local_heads * HEAD_DIM)
    grad_values = value_sum.reshape(local_tokens, local_heads * HEAD_DIM)
    return (attn_output, grad_queries, grad_keys, grad_values, grad_weight)


def solution(mesh):
    in_specs = (
        P("seq", "fsdp"),
        P("seq", "fsdp"),
        P("seq", "fsdp"),
        P("seq"),
        P("fsdp", "seq"),
        P("seq", "fsdp"),
    )
    out_specs = (
        P("seq", "fsdp"),
        P("seq", "fsdp"),
        P("seq", "fsdp"),
        P("seq", "fsdp"),
        P("fsdp", "seq"),
    )
    return jax.shard_map(shards, mesh=mesh, in_specs=in_specs, out_specs=out_specs, check_vma=False)
```

```python
import jax
import jax.numpy as jnp
from jax import lax
from jax.sharding import PartitionSpec as P

HEAD_DIM = 128


blocked = -1e30


def split_heads(matrix):
    return matrix.reshape(matrix.shape[0], -1, HEAD_DIM)


def masked_scores(query_rows, key_rows, query_pos, key_pos):
    raw = jnp.einsum(
        "qhd,khd->hqk", query_rows, key_rows, preferred_element_type=jnp.float32
    ) * HEAD_DIM ** (-0.5)
    visible = key_pos[None, None, :] <= query_pos[None, :, None]
    return jnp.where(visible, raw, blocked)


def shift_pieces(block, axis):
    count = lax.axis_size(axis)
    pieces = [block]
    for distance in range(1, count):
        route = [(i, (i + distance) % count) for i in range(count)]
        pieces.append(lax.ppermute(block, axis, route))
    return pieces


def permute_gather(block, axis, dim):
    count = lax.axis_size(axis)
    me = lax.axis_index(axis)
    width = block.shape[dim]
    shape = list(block.shape)
    shape[dim] = width * count
    full = jnp.zeros(shape, block.dtype)
    for distance, piece in enumerate(shift_pieces(block, axis)):
        start = [0] * block.ndim
        start[dim] = ((me - distance) % count) * width
        full = lax.dynamic_update_slice(full, piece, start)
    return full


def pair_gather(block, axis, dim):
    count = lax.axis_size(axis)
    if count % 2:
        return permute_gather(block, axis, dim)
    me = lax.axis_index(axis)
    mate = me + 1 - 2 * (me % 2)
    chips = count // 2
    width = block.shape[dim]
    shape = list(block.shape)
    shape[dim] = width * count
    full = jnp.zeros(shape, block.dtype)
    pair_route = [(i, i ^ 1) for i in range(count)]
    for step in range(chips):
        if step:
            route = [(i, (i + 2 * step) % count) for i in range(count)]
            piece = lax.ppermute(block, axis, route)
        else:
            piece = block
        mate_piece = lax.ppermute(piece, axis, pair_route)
        for source, part in (((me - 2 * step) % count, piece), ((mate - 2 * step) % count, mate_piece)):
            start = [0] * block.ndim
            start[dim] = source * width
            full = lax.dynamic_update_slice(full, part, start)
    return full


def permute_sum_scatter(block, axis, dim):
    count = lax.axis_size(axis)
    me = lax.axis_index(axis)
    width = block.shape[dim] // count
    total = lax.dynamic_slice_in_dim(block, me * width, width, dim).astype(jnp.float32)
    for distance in range(1, count):
        route = [(i, (i + distance) % count) for i in range(count)]
        piece = lax.dynamic_slice_in_dim(block, ((me + distance) % count) * width, width, dim)
        total = total + lax.ppermute(piece, axis, route).astype(jnp.float32)
    return total


def shards(query_states, key_states, value_states, positions, out_weight, cotangent):
    local_tokens = query_states.shape[0]
    query_heads = split_heads(query_states)
    local_heads = query_heads.shape[1]
    model_cols = key_states.shape[1]
    pos_cols = jnp.zeros((local_tokens, 128), jnp.bfloat16)
    pos_cols = pos_cols.at[:, 0].set((positions // 256).astype(jnp.bfloat16))
    pos_cols = pos_cols.at[:, 1].set((positions % 256).astype(jnp.bfloat16))
    packed = jnp.concatenate([key_states, value_states, pos_cols], axis=1)
    all_packed = lax.all_gather(packed, "seq", axis=0, tiled=True)
    all_keys = all_packed[:, :model_cols]
    all_values = all_packed[:, model_cols : 2 * model_cols]
    all_pos = all_packed[:, 2 * model_cols].astype(jnp.int32) * 256 + all_packed[
        :, 2 * model_cols + 1
    ].astype(jnp.int32)
    key_heads = split_heads(all_keys)
    value_heads = split_heads(all_values)
    scores = masked_scores(query_heads, key_heads, positions, all_pos)
    row_max = jnp.max(scores, axis=2)
    log_total = row_max + jnp.log(jnp.sum(jnp.exp(scores - row_max[:, :, None]), axis=2))
    probs = jnp.exp(scores - log_total[:, :, None])
    weights = probs.astype(jnp.bfloat16)
    attended = jnp.einsum(
        "hqk,khd->qhd", weights, value_heads, preferred_element_type=jnp.float32
    )
    attended_heads = attended.astype(jnp.bfloat16)
    attended_flat = attended_heads.reshape(local_tokens, local_heads * HEAD_DIM)
    weight_full = pair_gather(out_weight, "seq", 1)
    partial_sum = jnp.dot(attended_flat, weight_full, preferred_element_type=jnp.float32).astype(
        jnp.bfloat16
    )
    cotangent_full = permute_gather(cotangent, "fsdp", 1)
    grad_attended = jnp.einsum(
        "td,hd->th", cotangent_full, weight_full, preferred_element_type=jnp.float32
    ).astype(jnp.bfloat16)
    partial_sum, grad_attended = lax.optimization_barrier((partial_sum, grad_attended))
    attn_output = permute_sum_scatter(partial_sum, "fsdp", 1)
    all_attended = lax.all_gather(attended_flat, "seq", axis=0, tiled=True)
    cotangent_cols = lax.all_to_all(cotangent_full, "seq", 1, 0, tiled=True)
    grad_weight = jnp.einsum(
        "th,td->hd", all_attended, cotangent_cols, preferred_element_type=jnp.float32
    )
    grad_heads = split_heads(grad_attended)
    row_delta = jnp.sum(
        grad_heads.astype(jnp.float32) * attended_heads.astype(jnp.float32), axis=2
    ).T
    grad_probs = jnp.einsum(
        "qhd,khd->hqk", grad_heads, value_heads, preferred_element_type=jnp.float32
    )
    grad_scores = (probs * (grad_probs - row_delta[:, :, None])).astype(jnp.bfloat16)
    query_sum = jnp.einsum(
        "hqk,khd->qhd", grad_scores, key_heads, preferred_element_type=jnp.float32
    )
    key_part = jnp.einsum(
        "hqk,qhd->khd", grad_scores, query_heads, preferred_element_type=jnp.float32
    )
    value_part = jnp.einsum(
        "hqk,qhd->khd", weights, grad_heads, preferred_element_type=jnp.float32
    )
    both_parts = jnp.concatenate([key_part, value_part], axis=1).astype(jnp.bfloat16)
    both_sums = lax.psum_scatter(both_parts, "seq", scatter_dimension=0, tiled=True).astype(
        jnp.float32
    )
    key_sum = both_sums[:, :local_heads]
    value_sum = both_sums[:, local_heads:]
    score_scale = HEAD_DIM ** (-0.5)
    grad_queries = (query_sum * score_scale).reshape(local_tokens, local_heads * HEAD_DIM)
    grad_keys = (key_sum * score_scale).reshape(local_tokens, local_heads * HEAD_DIM)
    grad_values = value_sum.reshape(local_tokens, local_heads * HEAD_DIM)
    return (attn_output, grad_queries, grad_keys, grad_values, grad_weight)


def solution(mesh):
    in_specs = (
        P("seq", "fsdp"),
        P("seq", "fsdp"),
        P("seq", "fsdp"),
        P("seq"),
        P("fsdp", "seq"),
        P("seq", "fsdp"),
    )
    out_specs = (
        P("seq", "fsdp"),
        P("seq", "fsdp"),
        P("seq", "fsdp"),
        P("seq", "fsdp"),
        P("fsdp", "seq"),
    )
    return jax.shard_map(shards, mesh=mesh, in_specs=in_specs, out_specs=out_specs, check_vma=False)
```

```python
import jax
import jax.numpy as jnp
from jax import lax
from jax.sharding import PartitionSpec as P

HEAD_DIM = 128


blocked = -1e30


def split_heads(matrix):
    return matrix.reshape(matrix.shape[0], -1, HEAD_DIM)


def masked_scores(query_rows, key_rows, query_pos, key_pos):
    raw = jnp.einsum(
        "qhd,khd->hqk", query_rows, key_rows, preferred_element_type=jnp.float32
    ) * HEAD_DIM ** (-0.5)
    visible = key_pos[None, None, :] <= query_pos[None, :, None]
    return jnp.where(visible, raw, blocked)


def shift_pieces(block, axis):
    count = lax.axis_size(axis)
    pieces = [block]
    for distance in range(1, count):
        route = [(i, (i + distance) % count) for i in range(count)]
        pieces.append(lax.ppermute(block, axis, route))
    return pieces


def permute_gather(block, axis, dim):
    count = lax.axis_size(axis)
    me = lax.axis_index(axis)
    width = block.shape[dim]
    shape = list(block.shape)
    shape[dim] = width * count
    full = jnp.zeros(shape, block.dtype)
    for distance, piece in enumerate(shift_pieces(block, axis)):
        start = [0] * block.ndim
        start[dim] = ((me - distance) % count) * width
        full = lax.dynamic_update_slice(full, piece, start)
    return full


def permute_sum_scatter(block, axis, dim):
    count = lax.axis_size(axis)
    me = lax.axis_index(axis)
    width = block.shape[dim] // count
    total = lax.dynamic_slice_in_dim(block, me * width, width, dim).astype(jnp.float32)
    for distance in range(1, count):
        route = [(i, (i + distance) % count) for i in range(count)]
        piece = lax.dynamic_slice_in_dim(block, ((me + distance) % count) * width, width, dim)
        total = total + lax.ppermute(piece, axis, route).astype(jnp.float32)
    return total


def shards(query_states, key_states, value_states, positions, out_weight, cotangent):
    local_tokens = query_states.shape[0]
    query_heads = split_heads(query_states)
    local_heads = query_heads.shape[1]
    all_keys = lax.all_gather(key_states, "seq", axis=0, tiled=True)
    all_values = lax.all_gather(value_states, "seq", axis=0, tiled=True)
    all_pos = lax.all_gather(positions, "seq", axis=0, tiled=True)
    key_heads = split_heads(all_keys)
    value_heads = split_heads(all_values)
    scores = masked_scores(query_heads, key_heads, positions, all_pos)
    row_max = jnp.max(scores, axis=2)
    log_total = row_max + jnp.log(jnp.sum(jnp.exp(scores - row_max[:, :, None]), axis=2))
    probs = jnp.exp(scores - log_total[:, :, None])
    weights = probs.astype(jnp.bfloat16)
    attended = jnp.einsum(
        "hqk,khd->qhd", weights, value_heads, preferred_element_type=jnp.float32
    )
    attended_heads = attended.astype(jnp.bfloat16)
    attended_flat = attended_heads.reshape(local_tokens, local_heads * HEAD_DIM)
    weight_full = lax.all_gather(out_weight, "seq", axis=1, tiled=True)
    partial_sum = jnp.dot(attended_flat, weight_full, preferred_element_type=jnp.float32).astype(
        jnp.bfloat16
    )
    attn_output = permute_sum_scatter(partial_sum, "fsdp", 1)
    cotangent_full = permute_gather(cotangent, "fsdp", 1)
    grad_attended = jnp.einsum(
        "td,hd->th", cotangent_full, weight_full, preferred_element_type=jnp.float32
    ).astype(jnp.bfloat16)
    all_attended = lax.all_gather(attended_flat, "seq", axis=0, tiled=True)
    cotangent_cols = lax.all_to_all(cotangent_full, "seq", 1, 0, tiled=True)
    grad_weight = jnp.einsum(
        "th,td->hd", all_attended, cotangent_cols, preferred_element_type=jnp.float32
    )
    grad_heads = split_heads(grad_attended)
    row_delta = jnp.sum(
        grad_heads.astype(jnp.float32) * attended_heads.astype(jnp.float32), axis=2
    ).T
    grad_probs = jnp.einsum(
        "qhd,khd->hqk", grad_heads, value_heads, preferred_element_type=jnp.float32
    )
    grad_scores = (probs * (grad_probs - row_delta[:, :, None])).astype(jnp.bfloat16)
    query_sum = jnp.einsum(
        "hqk,khd->qhd", grad_scores, key_heads, preferred_element_type=jnp.float32
    )
    key_part = jnp.einsum(
        "hqk,qhd->khd", grad_scores, query_heads, preferred_element_type=jnp.float32
    )
    value_part = jnp.einsum(
        "hqk,qhd->khd", weights, grad_heads, preferred_element_type=jnp.float32
    )
    both_parts = jnp.concatenate([key_part, value_part], axis=1).astype(jnp.bfloat16)
    attn_output, both_parts = lax.optimization_barrier((attn_output, both_parts))
    both_sums = lax.psum_scatter(both_parts, "seq", scatter_dimension=0, tiled=True).astype(
        jnp.float32
    )
    key_sum = both_sums[:, :local_heads]
    value_sum = both_sums[:, local_heads:]
    score_scale = HEAD_DIM ** (-0.5)
    grad_queries = (query_sum * score_scale).reshape(local_tokens, local_heads * HEAD_DIM)
    grad_keys = (key_sum * score_scale).reshape(local_tokens, local_heads * HEAD_DIM)
    grad_values = value_sum.reshape(local_tokens, local_heads * HEAD_DIM)
    return (attn_output, grad_queries, grad_keys, grad_values, grad_weight)


def solution(mesh):
    in_specs = (
        P("seq", "fsdp"),
        P("seq", "fsdp"),
        P("seq", "fsdp"),
        P("seq"),
        P("fsdp", "seq"),
        P("seq", "fsdp"),
    )
    out_specs = (
        P("seq", "fsdp"),
        P("seq", "fsdp"),
        P("seq", "fsdp"),
        P("seq", "fsdp"),
        P("fsdp", "seq"),
    )
    return jax.shard_map(shards, mesh=mesh, in_specs=in_specs, out_specs=out_specs, check_vma=False)
```

```python
import jax
import jax.numpy as jnp
from jax import lax
from jax.sharding import PartitionSpec as P

HEAD_DIM = 128


blocked = -1e30


def split_heads(matrix):
    return matrix.reshape(matrix.shape[0], -1, HEAD_DIM)


def masked_scores(query_rows, key_rows, query_pos, key_pos):
    raw = jnp.einsum(
        "qhd,khd->hqk", query_rows, key_rows, preferred_element_type=jnp.float32
    ) * HEAD_DIM ** (-0.5)
    visible = key_pos[None, None, :] <= query_pos[None, :, None]
    return jnp.where(visible, raw, blocked)


def shift_pieces(block, axis):
    count = lax.axis_size(axis)
    pieces = [block]
    for distance in range(1, count):
        route = [(i, (i + distance) % count) for i in range(count)]
        pieces.append(lax.ppermute(block, axis, route))
    return pieces


def permute_gather(block, axis, dim):
    count = lax.axis_size(axis)
    me = lax.axis_index(axis)
    width = block.shape[dim]
    shape = list(block.shape)
    shape[dim] = width * count
    full = jnp.zeros(shape, block.dtype)
    for distance, piece in enumerate(shift_pieces(block, axis)):
        start = [0] * block.ndim
        start[dim] = ((me - distance) % count) * width
        full = lax.dynamic_update_slice(full, piece, start)
    return full


def permute_sum_scatter(block, axis, dim):
    count = lax.axis_size(axis)
    me = lax.axis_index(axis)
    width = block.shape[dim] // count
    total = lax.dynamic_slice_in_dim(block, me * width, width, dim).astype(jnp.float32)
    for distance in range(1, count):
        route = [(i, (i + distance) % count) for i in range(count)]
        piece = lax.dynamic_slice_in_dim(block, ((me + distance) % count) * width, width, dim)
        total = total + lax.ppermute(piece, axis, route).astype(jnp.float32)
    return total


def shards(query_states, key_states, value_states, positions, out_weight, cotangent):
    local_tokens = query_states.shape[0]
    query_heads = split_heads(query_states)
    local_heads = query_heads.shape[1]
    all_keys = lax.all_gather(key_states, "seq", axis=0, tiled=True)
    all_values = lax.all_gather(value_states, "seq", axis=0, tiled=True)
    all_pos = lax.all_gather(positions, "seq", axis=0, tiled=True)
    key_heads = split_heads(all_keys)
    value_heads = split_heads(all_values)
    scores = masked_scores(query_heads, key_heads, positions, all_pos)
    row_max = jnp.max(scores, axis=2)
    log_total = row_max + jnp.log(jnp.sum(jnp.exp(scores - row_max[:, :, None]), axis=2))
    probs = jnp.exp(scores - log_total[:, :, None])
    weights = probs.astype(jnp.bfloat16)
    attended = jnp.einsum(
        "hqk,khd->qhd", weights, value_heads, preferred_element_type=jnp.float32
    )
    attended_heads = attended.astype(jnp.bfloat16)
    attended_flat = attended_heads.reshape(local_tokens, local_heads * HEAD_DIM)
    weight_full = lax.all_gather(out_weight, "seq", axis=1, tiled=True)
    partial_sum = jnp.dot(attended_flat, weight_full, preferred_element_type=jnp.float32).astype(
        jnp.bfloat16
    )
    attn_output = permute_sum_scatter(partial_sum, "fsdp", 1)
    cotangent_full = permute_gather(cotangent, "fsdp", 1)
    grad_attended = jnp.einsum(
        "td,hd->th", cotangent_full, weight_full, preferred_element_type=jnp.float32
    ).astype(jnp.bfloat16)
    all_attended = lax.all_gather(attended_flat, "seq", axis=0, tiled=True)
    cotangent_cols = lax.all_to_all(cotangent_full, "seq", 1, 0, tiled=True)
    grad_weight = jnp.einsum(
        "th,td->hd", all_attended, cotangent_cols, preferred_element_type=jnp.float32
    )
    grad_heads = split_heads(grad_attended)
    row_delta = jnp.sum(
        grad_heads.astype(jnp.float32) * attended_heads.astype(jnp.float32), axis=2
    ).T
    halves = 2 if local_heads % 2 == 0 else 1
    span = local_heads // halves
    query_sums, key_sums, value_sums = [], [], []
    for half in range(halves):
        heads = slice(half * span, (half + 1) * span)
        half_grads = grad_heads[:, heads]
        grad_probs = jnp.einsum(
            "qhd,khd->hqk", half_grads, value_heads[:, heads], preferred_element_type=jnp.float32
        )
        grad_scores = (probs[heads] * (grad_probs - row_delta[heads, :, None])).astype(
            jnp.bfloat16
        )
        query_sums.append(
            jnp.einsum(
                "hqk,khd->qhd", grad_scores, key_heads[:, heads], preferred_element_type=jnp.float32
            )
        )
        key_part = jnp.einsum(
            "hqk,qhd->khd", grad_scores, query_heads[:, heads], preferred_element_type=jnp.float32
        )
        value_part = jnp.einsum(
            "hqk,qhd->khd", weights[heads], half_grads, preferred_element_type=jnp.float32
        )
        both_parts = jnp.concatenate([key_part, value_part], axis=1).astype(jnp.bfloat16)
        if half == 0:
            attn_output, both_parts = lax.optimization_barrier((attn_output, both_parts))
        both_sums = lax.psum_scatter(both_parts, "seq", scatter_dimension=0, tiled=True).astype(
            jnp.float32
        )
        key_sums.append(both_sums[:, :span])
        value_sums.append(both_sums[:, span:])
    query_sum = jnp.concatenate(query_sums, axis=1)
    key_sum = jnp.concatenate(key_sums, axis=1)
    value_sum = jnp.concatenate(value_sums, axis=1)
    score_scale = HEAD_DIM ** (-0.5)
    grad_queries = (query_sum * score_scale).reshape(local_tokens, local_heads * HEAD_DIM)
    grad_keys = (key_sum * score_scale).reshape(local_tokens, local_heads * HEAD_DIM)
    grad_values = value_sum.reshape(local_tokens, local_heads * HEAD_DIM)
    return (attn_output, grad_queries, grad_keys, grad_values, grad_weight)


def solution(mesh):
    in_specs = (
        P("seq", "fsdp"),
        P("seq", "fsdp"),
        P("seq", "fsdp"),
        P("seq"),
        P("fsdp", "seq"),
        P("seq", "fsdp"),
    )
    out_specs = (
        P("seq", "fsdp"),
        P("seq", "fsdp"),
        P("seq", "fsdp"),
        P("seq", "fsdp"),
        P("fsdp", "seq"),
    )
    return jax.shard_map(shards, mesh=mesh, in_specs=in_specs, out_specs=out_specs, check_vma=False)
```

```python
import jax
import jax.numpy as jnp
from jax import lax
from jax.sharding import PartitionSpec as P

HEAD_DIM = 128


blocked = -1e30


def split_heads(matrix):
    return matrix.reshape(matrix.shape[0], -1, HEAD_DIM)


def masked_scores(query_rows, key_rows, query_pos, key_pos):
    raw = jnp.einsum(
        "qhd,khd->hqk", query_rows, key_rows, preferred_element_type=jnp.float32
    ) * HEAD_DIM ** (-0.5)
    visible = key_pos[None, None, :] <= query_pos[None, :, None]
    return jnp.where(visible, raw, blocked)


def shift_pieces(block, axis):
    count = lax.axis_size(axis)
    pieces = [block]
    for distance in range(1, count):
        route = [(i, (i + distance) % count) for i in range(count)]
        pieces.append(lax.ppermute(block, axis, route))
    return pieces


def permute_gather(block, axis, dim):
    count = lax.axis_size(axis)
    me = lax.axis_index(axis)
    width = block.shape[dim]
    shape = list(block.shape)
    shape[dim] = width * count
    full = jnp.zeros(shape, block.dtype)
    for distance, piece in enumerate(shift_pieces(block, axis)):
        start = [0] * block.ndim
        start[dim] = ((me - distance) % count) * width
        full = lax.dynamic_update_slice(full, piece, start)
    return full


def permute_sum_scatter(block, axis, dim):
    count = lax.axis_size(axis)
    me = lax.axis_index(axis)
    width = block.shape[dim] // count
    total = lax.dynamic_slice_in_dim(block, me * width, width, dim).astype(jnp.float32)
    for distance in range(1, count):
        route = [(i, (i + distance) % count) for i in range(count)]
        piece = lax.dynamic_slice_in_dim(block, ((me + distance) % count) * width, width, dim)
        total = total + lax.ppermute(piece, axis, route).astype(jnp.float32)
    return total


def shards(query_states, key_states, value_states, positions, out_weight, cotangent):
    local_tokens = query_states.shape[0]
    query_heads = split_heads(query_states)
    local_heads = query_heads.shape[1]
    all_keys = lax.all_gather(key_states, "seq", axis=0, tiled=True)
    all_values = lax.all_gather(value_states, "seq", axis=0, tiled=True)
    all_pos = lax.all_gather(positions, "seq", axis=0, tiled=True)
    key_heads = split_heads(all_keys)
    value_heads = split_heads(all_values)
    scores = masked_scores(query_heads, key_heads, positions, all_pos)
    row_max = jnp.max(scores, axis=2)
    log_total = row_max + jnp.log(jnp.sum(jnp.exp(scores - row_max[:, :, None]), axis=2))
    probs = jnp.exp(scores - log_total[:, :, None])
    weights = probs.astype(jnp.bfloat16)
    attended = jnp.einsum(
        "hqk,khd->qhd", weights, value_heads, preferred_element_type=jnp.float32
    )
    attended_heads = attended.astype(jnp.bfloat16)
    attended_flat = attended_heads.reshape(local_tokens, local_heads * HEAD_DIM)
    weight_full = lax.all_gather(out_weight, "seq", axis=1, tiled=True)
    partial_sum = jnp.dot(attended_flat, weight_full, preferred_element_type=jnp.float32).astype(
        jnp.bfloat16
    )
    attn_output = permute_sum_scatter(partial_sum, "fsdp", 1)
    cotangent_full = permute_gather(cotangent, "fsdp", 1)
    grad_attended = jnp.einsum(
        "td,hd->th", cotangent_full, weight_full, preferred_element_type=jnp.float32
    ).astype(jnp.bfloat16)
    all_attended = lax.all_gather(attended_flat, "seq", axis=0, tiled=True)
    cotangent_cols = lax.all_to_all(cotangent_full, "seq", 1, 0, tiled=True)
    grad_heads = split_heads(grad_attended)
    row_delta = jnp.sum(
        grad_heads.astype(jnp.float32) * attended_heads.astype(jnp.float32), axis=2
    ).T
    halves = 2 if local_heads % 2 == 0 else 1
    span = local_heads // halves
    query_sums, key_sums, value_sums = [], [], []
    for half in range(halves):
        heads = slice(half * span, (half + 1) * span)
        half_grads = grad_heads[:, heads]
        grad_probs = jnp.einsum(
            "qhd,khd->hqk", half_grads, value_heads[:, heads], preferred_element_type=jnp.float32
        )
        grad_scores = (probs[heads] * (grad_probs - row_delta[heads, :, None])).astype(
            jnp.bfloat16
        )
        query_sums.append(
            jnp.einsum(
                "hqk,khd->qhd", grad_scores, key_heads[:, heads], preferred_element_type=jnp.float32
            )
        )
        key_part = jnp.einsum(
            "hqk,qhd->khd", grad_scores, query_heads[:, heads], preferred_element_type=jnp.float32
        )
        value_part = jnp.einsum(
            "hqk,qhd->khd", weights[heads], half_grads, preferred_element_type=jnp.float32
        )
        both_parts = jnp.concatenate([key_part, value_part], axis=1).astype(jnp.bfloat16)
        if half == 0:
            attn_output, all_attended, both_parts = lax.optimization_barrier(
                (attn_output, all_attended, both_parts)
            )
        both_sums = lax.psum_scatter(both_parts, "seq", scatter_dimension=0, tiled=True).astype(
            jnp.float32
        )
        key_sums.append(both_sums[:, :span])
        value_sums.append(both_sums[:, span:])
    grad_weight = jnp.einsum(
        "th,td->hd", all_attended, cotangent_cols, preferred_element_type=jnp.float32
    )
    query_sum = jnp.concatenate(query_sums, axis=1)
    key_sum = jnp.concatenate(key_sums, axis=1)
    value_sum = jnp.concatenate(value_sums, axis=1)
    score_scale = HEAD_DIM ** (-0.5)
    grad_queries = (query_sum * score_scale).reshape(local_tokens, local_heads * HEAD_DIM)
    grad_keys = (key_sum * score_scale).reshape(local_tokens, local_heads * HEAD_DIM)
    grad_values = value_sum.reshape(local_tokens, local_heads * HEAD_DIM)
    return (attn_output, grad_queries, grad_keys, grad_values, grad_weight)


def solution(mesh):
    in_specs = (
        P("seq", "fsdp"),
        P("seq", "fsdp"),
        P("seq", "fsdp"),
        P("seq"),
        P("fsdp", "seq"),
        P("seq", "fsdp"),
    )
    out_specs = (
        P("seq", "fsdp"),
        P("seq", "fsdp"),
        P("seq", "fsdp"),
        P("seq", "fsdp"),
        P("fsdp", "seq"),
    )
    return jax.shard_map(shards, mesh=mesh, in_specs=in_specs, out_specs=out_specs, check_vma=False)
```

```python
import jax
import jax.numpy as jnp
from jax import lax
from jax.sharding import PartitionSpec as P

HEAD_DIM = 128


blocked = -1e30


def split_heads(matrix):
    return matrix.reshape(matrix.shape[0], -1, HEAD_DIM)


def masked_scores(query_rows, key_rows, query_pos, key_pos):
    raw = jnp.einsum(
        "qhd,khd->hqk", query_rows, key_rows, preferred_element_type=jnp.float32
    ) * HEAD_DIM ** (-0.5)
    visible = key_pos[None, None, :] <= query_pos[None, :, None]
    return jnp.where(visible, raw, blocked)


def shift_pieces(block, axis):
    count = lax.axis_size(axis)
    pieces = [block]
    for distance in range(1, count):
        route = [(i, (i + distance) % count) for i in range(count)]
        pieces.append(lax.ppermute(block, axis, route))
    return pieces


def permute_gather(block, axis, dim):
    count = lax.axis_size(axis)
    me = lax.axis_index(axis)
    width = block.shape[dim]
    shape = list(block.shape)
    shape[dim] = width * count
    full = jnp.zeros(shape, block.dtype)
    for distance, piece in enumerate(shift_pieces(block, axis)):
        start = [0] * block.ndim
        start[dim] = ((me - distance) % count) * width
        full = lax.dynamic_update_slice(full, piece, start)
    return full


def permute_sum_scatter(block, axis, dim):
    count = lax.axis_size(axis)
    me = lax.axis_index(axis)
    width = block.shape[dim] // count
    total = lax.dynamic_slice_in_dim(block, me * width, width, dim).astype(jnp.float32)
    for distance in range(1, count):
        route = [(i, (i + distance) % count) for i in range(count)]
        piece = lax.dynamic_slice_in_dim(block, ((me + distance) % count) * width, width, dim)
        total = total + lax.ppermute(piece, axis, route).astype(jnp.float32)
    return total


def shards(query_states, key_states, value_states, positions, out_weight, cotangent):
    local_tokens = query_states.shape[0]
    query_heads = split_heads(query_states)
    local_heads = query_heads.shape[1]
    all_keys = lax.all_gather(key_states, "seq", axis=0, tiled=True)
    all_values = lax.all_gather(value_states, "seq", axis=0, tiled=True)
    all_pos = lax.all_gather(positions, "seq", axis=0, tiled=True)
    cotangent_full = permute_gather(cotangent, "fsdp", 1)
    cotangent_cols = lax.all_to_all(cotangent_full, "seq", 1, 0, tiled=True)
    cotangent_cols, all_values = lax.optimization_barrier((cotangent_cols, all_values))
    key_heads = split_heads(all_keys)
    value_heads = split_heads(all_values)
    scores = masked_scores(query_heads, key_heads, positions, all_pos)
    row_max = jnp.max(scores, axis=2)
    log_total = row_max + jnp.log(jnp.sum(jnp.exp(scores - row_max[:, :, None]), axis=2))
    probs = jnp.exp(scores - log_total[:, :, None])
    weights = probs.astype(jnp.bfloat16)
    attended = jnp.einsum(
        "hqk,khd->qhd", weights, value_heads, preferred_element_type=jnp.float32
    )
    attended_heads = attended.astype(jnp.bfloat16)
    attended_flat = attended_heads.reshape(local_tokens, local_heads * HEAD_DIM)
    weight_full = lax.all_gather(out_weight, "seq", axis=1, tiled=True)
    partial_sum = jnp.dot(attended_flat, weight_full, preferred_element_type=jnp.float32).astype(
        jnp.bfloat16
    )
    attn_output = permute_sum_scatter(partial_sum, "fsdp", 1)
    grad_attended = jnp.einsum(
        "td,hd->th", cotangent_full, weight_full, preferred_element_type=jnp.float32
    ).astype(jnp.bfloat16)
    all_attended = lax.all_gather(attended_flat, "seq", axis=0, tiled=True)
    grad_heads = split_heads(grad_attended)
    row_delta = jnp.sum(
        grad_heads.astype(jnp.float32) * attended_heads.astype(jnp.float32), axis=2
    ).T
    halves = 2 if local_heads % 2 == 0 else 1
    span = local_heads // halves
    query_sums, key_sums, value_sums = [], [], []
    for half in range(halves):
        heads = slice(half * span, (half + 1) * span)
        half_grads = grad_heads[:, heads]
        grad_probs = jnp.einsum(
            "qhd,khd->hqk", half_grads, value_heads[:, heads], preferred_element_type=jnp.float32
        )
        grad_scores = (probs[heads] * (grad_probs - row_delta[heads, :, None])).astype(
            jnp.bfloat16
        )
        query_sums.append(
            jnp.einsum(
                "hqk,khd->qhd", grad_scores, key_heads[:, heads], preferred_element_type=jnp.float32
            )
        )
        key_part = jnp.einsum(
            "hqk,qhd->khd", grad_scores, query_heads[:, heads], preferred_element_type=jnp.float32
        )
        value_part = jnp.einsum(
            "hqk,qhd->khd", weights[heads], half_grads, preferred_element_type=jnp.float32
        )
        both_parts = jnp.concatenate([key_part, value_part], axis=1).astype(jnp.bfloat16)
        if half == 0:
            attn_output, all_attended, both_parts = lax.optimization_barrier(
                (attn_output, all_attended, both_parts)
            )
        both_sums = lax.psum_scatter(both_parts, "seq", scatter_dimension=0, tiled=True).astype(
            jnp.float32
        )
        key_sums.append(both_sums[:, :span])
        value_sums.append(both_sums[:, span:])
    grad_weight = jnp.einsum(
        "th,td->hd", all_attended, cotangent_cols, preferred_element_type=jnp.float32
    )
    query_sum = jnp.concatenate(query_sums, axis=1)
    key_sum = jnp.concatenate(key_sums, axis=1)
    value_sum = jnp.concatenate(value_sums, axis=1)
    score_scale = HEAD_DIM ** (-0.5)
    grad_queries = (query_sum * score_scale).reshape(local_tokens, local_heads * HEAD_DIM)
    grad_keys = (key_sum * score_scale).reshape(local_tokens, local_heads * HEAD_DIM)
    grad_values = value_sum.reshape(local_tokens, local_heads * HEAD_DIM)
    return (attn_output, grad_queries, grad_keys, grad_values, grad_weight)


def solution(mesh):
    in_specs = (
        P("seq", "fsdp"),
        P("seq", "fsdp"),
        P("seq", "fsdp"),
        P("seq"),
        P("fsdp", "seq"),
        P("seq", "fsdp"),
    )
    out_specs = (
        P("seq", "fsdp"),
        P("seq", "fsdp"),
        P("seq", "fsdp"),
        P("seq", "fsdp"),
        P("fsdp", "seq"),
    )
    return jax.shard_map(shards, mesh=mesh, in_specs=in_specs, out_specs=out_specs, check_vma=False)
```

```python
import jax
import jax.numpy as jnp
from jax import lax
from jax.sharding import PartitionSpec as P

HEAD_DIM = 128


blocked = -1e30


def split_heads(matrix):
    return matrix.reshape(matrix.shape[0], -1, HEAD_DIM)


def masked_scores(query_rows, key_rows, query_pos, key_pos):
    raw = jnp.einsum(
        "qhd,khd->hqk", query_rows, key_rows, preferred_element_type=jnp.float32
    ) * HEAD_DIM ** (-0.5)
    visible = key_pos[None, None, :] <= query_pos[None, :, None]
    return jnp.where(visible, raw, blocked)


def shift_pieces(block, axis):
    count = lax.axis_size(axis)
    pieces = [block]
    for distance in range(1, count):
        route = [(i, (i + distance) % count) for i in range(count)]
        pieces.append(lax.ppermute(block, axis, route))
    return pieces


def permute_gather(block, axis, dim):
    count = lax.axis_size(axis)
    me = lax.axis_index(axis)
    width = block.shape[dim]
    shape = list(block.shape)
    shape[dim] = width * count
    full = jnp.zeros(shape, block.dtype)
    for distance, piece in enumerate(shift_pieces(block, axis)):
        start = [0] * block.ndim
        start[dim] = ((me - distance) % count) * width
        full = lax.dynamic_update_slice(full, piece, start)
    return full


def permute_sum_scatter(block, axis, dim):
    count = lax.axis_size(axis)
    me = lax.axis_index(axis)
    width = block.shape[dim] // count
    total = lax.dynamic_slice_in_dim(block, me * width, width, dim).astype(jnp.float32)
    for distance in range(1, count):
        route = [(i, (i + distance) % count) for i in range(count)]
        piece = lax.dynamic_slice_in_dim(block, ((me + distance) % count) * width, width, dim)
        total = total + lax.ppermute(piece, axis, route).astype(jnp.float32)
    return total


def shards(query_states, key_states, value_states, positions, out_weight, cotangent):
    local_tokens = query_states.shape[0]
    query_heads = split_heads(query_states)
    local_heads = query_heads.shape[1]
    model_cols = key_states.shape[1]
    packed = jnp.concatenate([key_states, value_states], axis=1)
    all_packed = lax.all_gather(packed, "seq", axis=0, tiled=True)
    all_keys = all_packed[:, :model_cols]
    all_values = all_packed[:, model_cols:]
    all_pos = lax.all_gather(positions, "seq", axis=0, tiled=True)
    key_heads = split_heads(all_keys)
    value_heads = split_heads(all_values)
    scores = masked_scores(query_heads, key_heads, positions, all_pos)
    row_max = jnp.max(scores, axis=2)
    log_total = row_max + jnp.log(jnp.sum(jnp.exp(scores - row_max[:, :, None]), axis=2))
    probs = jnp.exp(scores - log_total[:, :, None])
    weights = probs.astype(jnp.bfloat16)
    attended = jnp.einsum(
        "hqk,khd->qhd", weights, value_heads, preferred_element_type=jnp.float32
    )
    attended_heads = attended.astype(jnp.bfloat16)
    attended_flat = attended_heads.reshape(local_tokens, local_heads * HEAD_DIM)
    weight_full = lax.all_gather(out_weight, "seq", axis=1, tiled=True)
    partial_sum = jnp.dot(attended_flat, weight_full, preferred_element_type=jnp.float32).astype(
        jnp.bfloat16
    )
    attn_output = permute_sum_scatter(partial_sum, "fsdp", 1)
    cotangent_full = permute_gather(cotangent, "fsdp", 1)
    grad_attended = jnp.einsum(
        "td,hd->th", cotangent_full, weight_full, preferred_element_type=jnp.float32
    ).astype(jnp.bfloat16)
    all_attended = lax.all_gather(attended_flat, "seq", axis=0, tiled=True)
    cotangent_cols = lax.all_to_all(cotangent_full, "seq", 1, 0, tiled=True)
    grad_heads = split_heads(grad_attended)
    row_delta = jnp.sum(
        grad_heads.astype(jnp.float32) * attended_heads.astype(jnp.float32), axis=2
    ).T
    halves = 2 if local_heads % 2 == 0 else 1
    span = local_heads // halves
    query_sums, key_sums, value_sums = [], [], []
    for half in range(halves):
        heads = slice(half * span, (half + 1) * span)
        half_grads = grad_heads[:, heads]
        grad_probs = jnp.einsum(
            "qhd,khd->hqk", half_grads, value_heads[:, heads], preferred_element_type=jnp.float32
        )
        grad_scores = (probs[heads] * (grad_probs - row_delta[heads, :, None])).astype(
            jnp.bfloat16
        )
        query_sums.append(
            jnp.einsum(
                "hqk,khd->qhd", grad_scores, key_heads[:, heads], preferred_element_type=jnp.float32
            )
        )
        key_part = jnp.einsum(
            "hqk,qhd->khd", grad_scores, query_heads[:, heads], preferred_element_type=jnp.float32
        )
        value_part = jnp.einsum(
            "hqk,qhd->khd", weights[heads], half_grads, preferred_element_type=jnp.float32
        )
        both_parts = jnp.concatenate([key_part, value_part], axis=1).astype(jnp.bfloat16)
        if half == 0:
            attn_output, all_attended, both_parts = lax.optimization_barrier(
                (attn_output, all_attended, both_parts)
            )
        both_sums = lax.psum_scatter(both_parts, "seq", scatter_dimension=0, tiled=True).astype(
            jnp.float32
        )
        key_sums.append(both_sums[:, :span])
        value_sums.append(both_sums[:, span:])
    grad_weight = jnp.einsum(
        "th,td->hd", all_attended, cotangent_cols, preferred_element_type=jnp.float32
    )
    query_sum = jnp.concatenate(query_sums, axis=1)
    key_sum = jnp.concatenate(key_sums, axis=1)
    value_sum = jnp.concatenate(value_sums, axis=1)
    score_scale = HEAD_DIM ** (-0.5)
    grad_queries = (query_sum * score_scale).reshape(local_tokens, local_heads * HEAD_DIM)
    grad_keys = (key_sum * score_scale).reshape(local_tokens, local_heads * HEAD_DIM)
    grad_values = value_sum.reshape(local_tokens, local_heads * HEAD_DIM)
    return (attn_output, grad_queries, grad_keys, grad_values, grad_weight)


def solution(mesh):
    in_specs = (
        P("seq", "fsdp"),
        P("seq", "fsdp"),
        P("seq", "fsdp"),
        P("seq"),
        P("fsdp", "seq"),
        P("seq", "fsdp"),
    )
    out_specs = (
        P("seq", "fsdp"),
        P("seq", "fsdp"),
        P("seq", "fsdp"),
        P("seq", "fsdp"),
        P("fsdp", "seq"),
    )
    return jax.shard_map(shards, mesh=mesh, in_specs=in_specs, out_specs=out_specs, check_vma=False)
```

```python
import jax
import jax.numpy as jnp
from jax import lax
from jax.sharding import PartitionSpec as P

HEAD_DIM = 128


blocked = -1e30


def split_heads(matrix):
    return matrix.reshape(matrix.shape[0], -1, HEAD_DIM)


def masked_scores(query_rows, key_rows, query_pos, key_pos):
    raw = jnp.einsum(
        "qhd,khd->hqk", query_rows, key_rows, preferred_element_type=jnp.float32
    ) * HEAD_DIM ** (-0.5)
    visible = key_pos[None, None, :] <= query_pos[None, :, None]
    return jnp.where(visible, raw, blocked)


def shift_pieces(block, axis):
    count = lax.axis_size(axis)
    pieces = [block]
    for distance in range(1, count):
        route = [(i, (i + distance) % count) for i in range(count)]
        pieces.append(lax.ppermute(block, axis, route))
    return pieces


def permute_gather(block, axis, dim):
    count = lax.axis_size(axis)
    me = lax.axis_index(axis)
    width = block.shape[dim]
    shape = list(block.shape)
    shape[dim] = width * count
    full = jnp.zeros(shape, block.dtype)
    for distance, piece in enumerate(shift_pieces(block, axis)):
        start = [0] * block.ndim
        start[dim] = ((me - distance) % count) * width
        full = lax.dynamic_update_slice(full, piece, start)
    return full


def permute_sum_scatter(block, axis, dim):
    count = lax.axis_size(axis)
    me = lax.axis_index(axis)
    width = block.shape[dim] // count
    total = lax.dynamic_slice_in_dim(block, me * width, width, dim).astype(jnp.float32)
    for distance in range(1, count):
        route = [(i, (i + distance) % count) for i in range(count)]
        piece = lax.dynamic_slice_in_dim(block, ((me + distance) % count) * width, width, dim)
        total = total + lax.ppermute(piece, axis, route).astype(jnp.float32)
    return total


def shards(query_states, key_states, value_states, positions, out_weight, cotangent):
    local_tokens = query_states.shape[0]
    query_heads = split_heads(query_states)
    local_heads = query_heads.shape[1]
    model_cols = key_states.shape[1]
    seq_count = lax.axis_size("seq")
    packed = jnp.concatenate([key_states, value_states], axis=1)
    flat = jnp.concatenate([packed.reshape(-1), out_weight.reshape(-1)])
    all_flat = lax.all_gather(flat, "seq", axis=0, tiled=False)
    all_packed = all_flat[:, : packed.size].reshape(seq_count * local_tokens, 2 * model_cols)
    all_keys = all_packed[:, :model_cols]
    all_values = all_packed[:, model_cols:]
    weight_blocks = all_flat[:, packed.size :].reshape((seq_count,) + out_weight.shape)
    weight_full = weight_blocks.transpose(1, 0, 2).reshape(out_weight.shape[0], -1)
    all_pos = lax.all_gather(positions, "seq", axis=0, tiled=True)
    key_heads = split_heads(all_keys)
    value_heads = split_heads(all_values)
    scores = masked_scores(query_heads, key_heads, positions, all_pos)
    row_max = jnp.max(scores, axis=2)
    log_total = row_max + jnp.log(jnp.sum(jnp.exp(scores - row_max[:, :, None]), axis=2))
    probs = jnp.exp(scores - log_total[:, :, None])
    weights = probs.astype(jnp.bfloat16)
    attended = jnp.einsum(
        "hqk,khd->qhd", weights, value_heads, preferred_element_type=jnp.float32
    )
    attended_heads = attended.astype(jnp.bfloat16)
    attended_flat = attended_heads.reshape(local_tokens, local_heads * HEAD_DIM)
    partial_sum = jnp.dot(attended_flat, weight_full, preferred_element_type=jnp.float32).astype(
        jnp.bfloat16
    )
    attn_output = permute_sum_scatter(partial_sum, "fsdp", 1)
    cotangent_full = permute_gather(cotangent, "fsdp", 1)
    grad_attended = jnp.einsum(
        "td,hd->th", cotangent_full, weight_full, preferred_element_type=jnp.float32
    ).astype(jnp.bfloat16)
    all_attended = lax.all_gather(attended_flat, "seq", axis=0, tiled=True)
    cotangent_cols = lax.all_to_all(cotangent_full, "seq", 1, 0, tiled=True)
    grad_heads = split_heads(grad_attended)
    row_delta = jnp.sum(
        grad_heads.astype(jnp.float32) * attended_heads.astype(jnp.float32), axis=2
    ).T
    halves = 2 if local_heads % 2 == 0 else 1
    span = local_heads // halves
    query_sums, key_sums, value_sums = [], [], []
    for half in range(halves):
        heads = slice(half * span, (half + 1) * span)
        half_grads = grad_heads[:, heads]
        grad_probs = jnp.einsum(
            "qhd,khd->hqk", half_grads, value_heads[:, heads], preferred_element_type=jnp.float32
        )
        grad_scores = (probs[heads] * (grad_probs - row_delta[heads, :, None])).astype(
            jnp.bfloat16
        )
        query_sums.append(
            jnp.einsum(
                "hqk,khd->qhd", grad_scores, key_heads[:, heads], preferred_element_type=jnp.float32
            )
        )
        key_part = jnp.einsum(
            "hqk,qhd->khd", grad_scores, query_heads[:, heads], preferred_element_type=jnp.float32
        )
        value_part = jnp.einsum(
            "hqk,qhd->khd", weights[heads], half_grads, preferred_element_type=jnp.float32
        )
        both_parts = jnp.concatenate([key_part, value_part], axis=1).astype(jnp.bfloat16)
        if half == 0:
            attn_output, all_attended, both_parts = lax.optimization_barrier(
                (attn_output, all_attended, both_parts)
            )
        both_sums = lax.psum_scatter(both_parts, "seq", scatter_dimension=0, tiled=True).astype(
            jnp.float32
        )
        key_sums.append(both_sums[:, :span])
        value_sums.append(both_sums[:, span:])
    grad_weight = jnp.einsum(
        "th,td->hd", all_attended, cotangent_cols, preferred_element_type=jnp.float32
    )
    query_sum = jnp.concatenate(query_sums, axis=1)
    key_sum = jnp.concatenate(key_sums, axis=1)
    value_sum = jnp.concatenate(value_sums, axis=1)
    score_scale = HEAD_DIM ** (-0.5)
    grad_queries = (query_sum * score_scale).reshape(local_tokens, local_heads * HEAD_DIM)
    grad_keys = (key_sum * score_scale).reshape(local_tokens, local_heads * HEAD_DIM)
    grad_values = value_sum.reshape(local_tokens, local_heads * HEAD_DIM)
    return (attn_output, grad_queries, grad_keys, grad_values, grad_weight)


def solution(mesh):
    in_specs = (
        P("seq", "fsdp"),
        P("seq", "fsdp"),
        P("seq", "fsdp"),
        P("seq"),
        P("fsdp", "seq"),
        P("seq", "fsdp"),
    )
    out_specs = (
        P("seq", "fsdp"),
        P("seq", "fsdp"),
        P("seq", "fsdp"),
        P("seq", "fsdp"),
        P("fsdp", "seq"),
    )
    return jax.shard_map(shards, mesh=mesh, in_specs=in_specs, out_specs=out_specs, check_vma=False)
```

```python
import jax
import jax.numpy as jnp
from jax import lax
from jax.sharding import PartitionSpec as P

HEAD_DIM = 128


blocked = -1e30


def split_heads(matrix):
    return matrix.reshape(matrix.shape[0], -1, HEAD_DIM)


def masked_scores(query_rows, key_rows, query_pos, key_pos):
    raw = jnp.einsum(
        "qhd,khd->hqk", query_rows, key_rows, preferred_element_type=jnp.float32
    ) * HEAD_DIM ** (-0.5)
    visible = key_pos[None, None, :] <= query_pos[None, :, None]
    return jnp.where(visible, raw, blocked)


def shift_pieces(block, axis):
    count = lax.axis_size(axis)
    pieces = [block]
    for distance in range(1, count):
        route = [(i, (i + distance) % count) for i in range(count)]
        pieces.append(lax.ppermute(block, axis, route))
    return pieces


def permute_gather(block, axis, dim):
    count = lax.axis_size(axis)
    me = lax.axis_index(axis)
    width = block.shape[dim]
    shape = list(block.shape)
    shape[dim] = width * count
    full = jnp.zeros(shape, block.dtype)
    for distance, piece in enumerate(shift_pieces(block, axis)):
        start = [0] * block.ndim
        start[dim] = ((me - distance) % count) * width
        full = lax.dynamic_update_slice(full, piece, start)
    return full


def pair_gather(block, axis, dim):
    count = lax.axis_size(axis)
    if count % 2:
        return permute_gather(block, axis, dim)
    me = lax.axis_index(axis)
    mate = me + 1 - 2 * (me % 2)
    chips = count // 2
    width = block.shape[dim]
    shape = list(block.shape)
    shape[dim] = width * count
    full = jnp.zeros(shape, block.dtype)
    pair_route = [(i, i ^ 1) for i in range(count)]
    for step in range(chips):
        if step:
            route = [(i, (i + 2 * step) % count) for i in range(count)]
            piece = lax.ppermute(block, axis, route)
        else:
            piece = block
        mate_piece = lax.ppermute(piece, axis, pair_route)
        for source, part in (((me - 2 * step) % count, piece), ((mate - 2 * step) % count, mate_piece)):
            start = [0] * block.ndim
            start[dim] = source * width
            full = lax.dynamic_update_slice(full, part, start)
    return full


def permute_sum_scatter(block, axis, dim):
    count = lax.axis_size(axis)
    me = lax.axis_index(axis)
    width = block.shape[dim] // count
    total = lax.dynamic_slice_in_dim(block, me * width, width, dim).astype(jnp.float32)
    for distance in range(1, count):
        route = [(i, (i + distance) % count) for i in range(count)]
        piece = lax.dynamic_slice_in_dim(block, ((me + distance) % count) * width, width, dim)
        total = total + lax.ppermute(piece, axis, route).astype(jnp.float32)
    return total


def shards(query_states, key_states, value_states, positions, out_weight, cotangent):
    local_tokens = query_states.shape[0]
    query_heads = split_heads(query_states)
    local_heads = query_heads.shape[1]
    model_cols = key_states.shape[1]
    packed = jnp.concatenate([key_states, value_states], axis=1)
    all_packed = lax.all_gather(packed, "seq", axis=0, tiled=True)
    all_keys = all_packed[:, :model_cols]
    all_values = all_packed[:, model_cols:]
    all_pos = lax.all_gather(positions, "seq", axis=0, tiled=True)
    key_heads = split_heads(all_keys)
    value_heads = split_heads(all_values)
    scores = masked_scores(query_heads, key_heads, positions, all_pos)
    row_max = jnp.max(scores, axis=2)
    log_total = row_max + jnp.log(jnp.sum(jnp.exp(scores - row_max[:, :, None]), axis=2))
    probs = jnp.exp(scores - log_total[:, :, None])
    weights = probs.astype(jnp.bfloat16)
    attended = jnp.einsum(
        "hqk,khd->qhd", weights, value_heads, preferred_element_type=jnp.float32
    )
    attended_heads = attended.astype(jnp.bfloat16)
    attended_flat = attended_heads.reshape(local_tokens, local_heads * HEAD_DIM)
    weight_full = lax.all_gather(out_weight, "seq", axis=1, tiled=True)
    partial_sum = jnp.dot(attended_flat, weight_full, preferred_element_type=jnp.float32).astype(
        jnp.bfloat16
    )
    attn_output = permute_sum_scatter(partial_sum, "fsdp", 1)
    cotangent_full = permute_gather(cotangent, "fsdp", 1)
    grad_attended = jnp.einsum(
        "td,hd->th", cotangent_full, weight_full, preferred_element_type=jnp.float32
    ).astype(jnp.bfloat16)
    all_attended = pair_gather(attended_flat, "seq", 0)
    cotangent_cols = lax.all_to_all(cotangent_full, "seq", 1, 0, tiled=True)
    grad_heads = split_heads(grad_attended)
    row_delta = jnp.sum(
        grad_heads.astype(jnp.float32) * attended_heads.astype(jnp.float32), axis=2
    ).T
    halves = 2 if local_heads % 2 == 0 else 1
    span = local_heads // halves
    query_sums, key_sums, value_sums = [], [], []
    for half in range(halves):
        heads = slice(half * span, (half + 1) * span)
        half_grads = grad_heads[:, heads]
        grad_probs = jnp.einsum(
            "qhd,khd->hqk", half_grads, value_heads[:, heads], preferred_element_type=jnp.float32
        )
        grad_scores = (probs[heads] * (grad_probs - row_delta[heads, :, None])).astype(
            jnp.bfloat16
        )
        query_sums.append(
            jnp.einsum(
                "hqk,khd->qhd", grad_scores, key_heads[:, heads], preferred_element_type=jnp.float32
            )
        )
        key_part = jnp.einsum(
            "hqk,qhd->khd", grad_scores, query_heads[:, heads], preferred_element_type=jnp.float32
        )
        value_part = jnp.einsum(
            "hqk,qhd->khd", weights[heads], half_grads, preferred_element_type=jnp.float32
        )
        both_parts = jnp.concatenate([key_part, value_part], axis=1).astype(jnp.bfloat16)
        if half == 0:
            attn_output, all_attended, both_parts = lax.optimization_barrier(
                (attn_output, all_attended, both_parts)
            )
        both_sums = lax.psum_scatter(both_parts, "seq", scatter_dimension=0, tiled=True).astype(
            jnp.float32
        )
        key_sums.append(both_sums[:, :span])
        value_sums.append(both_sums[:, span:])
    grad_weight = jnp.einsum(
        "th,td->hd", all_attended, cotangent_cols, preferred_element_type=jnp.float32
    )
    query_sum = jnp.concatenate(query_sums, axis=1)
    key_sum = jnp.concatenate(key_sums, axis=1)
    value_sum = jnp.concatenate(value_sums, axis=1)
    score_scale = HEAD_DIM ** (-0.5)
    grad_queries = (query_sum * score_scale).reshape(local_tokens, local_heads * HEAD_DIM)
    grad_keys = (key_sum * score_scale).reshape(local_tokens, local_heads * HEAD_DIM)
    grad_values = value_sum.reshape(local_tokens, local_heads * HEAD_DIM)
    return (attn_output, grad_queries, grad_keys, grad_values, grad_weight)


def solution(mesh):
    in_specs = (
        P("seq", "fsdp"),
        P("seq", "fsdp"),
        P("seq", "fsdp"),
        P("seq"),
        P("fsdp", "seq"),
        P("seq", "fsdp"),
    )
    out_specs = (
        P("seq", "fsdp"),
        P("seq", "fsdp"),
        P("seq", "fsdp"),
        P("seq", "fsdp"),
        P("fsdp", "seq"),
    )
    return jax.shard_map(shards, mesh=mesh, in_specs=in_specs, out_specs=out_specs, check_vma=False)
```

```python
import jax
import jax.numpy as jnp
from jax import lax
from jax.sharding import PartitionSpec as P

HEAD_DIM = 128


blocked = -1e30


def split_heads(matrix):
    return matrix.reshape(matrix.shape[0], -1, HEAD_DIM)


def masked_scores(query_rows, key_rows, query_pos, key_pos):
    raw = jnp.einsum(
        "qhd,khd->hqk", query_rows, key_rows, preferred_element_type=jnp.float32
    ) * HEAD_DIM ** (-0.5)
    visible = key_pos[None, None, :] <= query_pos[None, :, None]
    return jnp.where(visible, raw, blocked)


def shift_pieces(block, axis):
    count = lax.axis_size(axis)
    pieces = [block]
    for distance in range(1, count):
        route = [(i, (i + distance) % count) for i in range(count)]
        pieces.append(lax.ppermute(block, axis, route))
    return pieces


def permute_gather(block, axis, dim):
    count = lax.axis_size(axis)
    me = lax.axis_index(axis)
    width = block.shape[dim]
    shape = list(block.shape)
    shape[dim] = width * count
    full = jnp.zeros(shape, block.dtype)
    for distance, piece in enumerate(shift_pieces(block, axis)):
        start = [0] * block.ndim
        start[dim] = ((me - distance) % count) * width
        full = lax.dynamic_update_slice(full, piece, start)
    return full


def pair_gather(block, axis, dim):
    count = lax.axis_size(axis)
    if count % 2:
        return permute_gather(block, axis, dim)
    me = lax.axis_index(axis)
    mate = me + 1 - 2 * (me % 2)
    chips = count // 2
    width = block.shape[dim]
    shape = list(block.shape)
    shape[dim] = width * count
    full = jnp.zeros(shape, block.dtype)
    pair_route = [(i, i ^ 1) for i in range(count)]
    for step in range(chips):
        if step:
            route = [(i, (i + 2 * step) % count) for i in range(count)]
            piece = lax.ppermute(block, axis, route)
        else:
            piece = block
        mate_piece = lax.ppermute(piece, axis, pair_route)
        for source, part in (((me - 2 * step) % count, piece), ((mate - 2 * step) % count, mate_piece)):
            start = [0] * block.ndim
            start[dim] = source * width
            full = lax.dynamic_update_slice(full, part, start)
    return full


def permute_sum_scatter(block, axis, dim):
    count = lax.axis_size(axis)
    me = lax.axis_index(axis)
    width = block.shape[dim] // count
    total = lax.dynamic_slice_in_dim(block, me * width, width, dim).astype(jnp.float32)
    for distance in range(1, count):
        route = [(i, (i + distance) % count) for i in range(count)]
        piece = lax.dynamic_slice_in_dim(block, ((me + distance) % count) * width, width, dim)
        total = total + lax.ppermute(piece, axis, route).astype(jnp.float32)
    return total


def shards(query_states, key_states, value_states, positions, out_weight, cotangent):
    local_tokens = query_states.shape[0]
    query_heads = split_heads(query_states)
    local_heads = query_heads.shape[1]
    model_cols = key_states.shape[1]
    packed = jnp.concatenate([key_states, value_states], axis=1)
    all_packed = lax.all_gather(packed, "seq", axis=0, tiled=True)
    all_keys = all_packed[:, :model_cols]
    all_values = all_packed[:, model_cols:]
    all_pos = lax.all_gather(positions, "seq", axis=0, tiled=True)
    key_heads = split_heads(all_keys)
    value_heads = split_heads(all_values)
    scores = masked_scores(query_heads, key_heads, positions, all_pos)
    row_max = jnp.max(scores, axis=2)
    log_total = row_max + jnp.log(jnp.sum(jnp.exp(scores - row_max[:, :, None]), axis=2))
    probs = jnp.exp(scores - log_total[:, :, None])
    weights = probs.astype(jnp.bfloat16)
    attended = jnp.einsum(
        "hqk,khd->qhd", weights, value_heads, preferred_element_type=jnp.float32
    )
    attended_heads = attended.astype(jnp.bfloat16)
    attended_flat = attended_heads.reshape(local_tokens, local_heads * HEAD_DIM)
    weight_full = pair_gather(out_weight, "seq", 1)
    partial_sum = jnp.dot(attended_flat, weight_full, preferred_element_type=jnp.float32).astype(
        jnp.bfloat16
    )
    attn_output = permute_sum_scatter(partial_sum, "fsdp", 1)
    cotangent_full = permute_gather(cotangent, "fsdp", 1)
    grad_attended = jnp.einsum(
        "td,hd->th", cotangent_full, weight_full, preferred_element_type=jnp.float32
    ).astype(jnp.bfloat16)
    all_attended = lax.all_gather(attended_flat, "seq", axis=0, tiled=True)
    cotangent_cols = lax.all_to_all(cotangent_full, "seq", 1, 0, tiled=True)
    grad_heads = split_heads(grad_attended)
    row_delta = jnp.sum(
        grad_heads.astype(jnp.float32) * attended_heads.astype(jnp.float32), axis=2
    ).T
    halves = 2 if local_heads % 2 == 0 else 1
    span = local_heads // halves
    query_sums, key_sums, value_sums = [], [], []
    for half in range(halves):
        heads = slice(half * span, (half + 1) * span)
        half_grads = grad_heads[:, heads]
        grad_probs = jnp.einsum(
            "qhd,khd->hqk", half_grads, value_heads[:, heads], preferred_element_type=jnp.float32
        )
        grad_scores = (probs[heads] * (grad_probs - row_delta[heads, :, None])).astype(
            jnp.bfloat16
        )
        query_sums.append(
            jnp.einsum(
                "hqk,khd->qhd", grad_scores, key_heads[:, heads], preferred_element_type=jnp.float32
            )
        )
        key_part = jnp.einsum(
            "hqk,qhd->khd", grad_scores, query_heads[:, heads], preferred_element_type=jnp.float32
        )
        value_part = jnp.einsum(
            "hqk,qhd->khd", weights[heads], half_grads, preferred_element_type=jnp.float32
        )
        both_parts = jnp.concatenate([key_part, value_part], axis=1).astype(jnp.bfloat16)
        if half == 0:
            attn_output, all_attended, both_parts = lax.optimization_barrier(
                (attn_output, all_attended, both_parts)
            )
        both_sums = lax.psum_scatter(both_parts, "seq", scatter_dimension=0, tiled=True).astype(
            jnp.float32
        )
        key_sums.append(both_sums[:, :span])
        value_sums.append(both_sums[:, span:])
    grad_weight = jnp.einsum(
        "th,td->hd", all_attended, cotangent_cols, preferred_element_type=jnp.float32
    )
    query_sum = jnp.concatenate(query_sums, axis=1)
    key_sum = jnp.concatenate(key_sums, axis=1)
    value_sum = jnp.concatenate(value_sums, axis=1)
    score_scale = HEAD_DIM ** (-0.5)
    grad_queries = (query_sum * score_scale).reshape(local_tokens, local_heads * HEAD_DIM)
    grad_keys = (key_sum * score_scale).reshape(local_tokens, local_heads * HEAD_DIM)
    grad_values = value_sum.reshape(local_tokens, local_heads * HEAD_DIM)
    return (attn_output, grad_queries, grad_keys, grad_values, grad_weight)


def solution(mesh):
    in_specs = (
        P("seq", "fsdp"),
        P("seq", "fsdp"),
        P("seq", "fsdp"),
        P("seq"),
        P("fsdp", "seq"),
        P("seq", "fsdp"),
    )
    out_specs = (
        P("seq", "fsdp"),
        P("seq", "fsdp"),
        P("seq", "fsdp"),
        P("seq", "fsdp"),
        P("fsdp", "seq"),
    )
    return jax.shard_map(shards, mesh=mesh, in_specs=in_specs, out_specs=out_specs, check_vma=False)
```

```python
import jax
import jax.numpy as jnp
from jax import lax
from jax.sharding import PartitionSpec as P

HEAD_DIM = 128


blocked = -1e30


def split_heads(matrix):
    return matrix.reshape(matrix.shape[0], -1, HEAD_DIM)


def masked_scores(query_rows, key_rows, query_pos, key_pos):
    raw = jnp.einsum(
        "qhd,khd->hqk", query_rows, key_rows, preferred_element_type=jnp.float32
    ) * HEAD_DIM ** (-0.5)
    visible = key_pos[None, None, :] <= query_pos[None, :, None]
    return jnp.where(visible, raw, blocked)


def shift_pieces(block, axis):
    count = lax.axis_size(axis)
    pieces = [block]
    for distance in range(1, count):
        route = [(i, (i + distance) % count) for i in range(count)]
        pieces.append(lax.ppermute(block, axis, route))
    return pieces


def permute_gather(block, axis, dim):
    count = lax.axis_size(axis)
    me = lax.axis_index(axis)
    width = block.shape[dim]
    shape = list(block.shape)
    shape[dim] = width * count
    full = jnp.zeros(shape, block.dtype)
    for distance, piece in enumerate(shift_pieces(block, axis)):
        start = [0] * block.ndim
        start[dim] = ((me - distance) % count) * width
        full = lax.dynamic_update_slice(full, piece, start)
    return full


def permute_sum_scatter(block, axis, dim):
    count = lax.axis_size(axis)
    me = lax.axis_index(axis)
    width = block.shape[dim] // count
    total = lax.dynamic_slice_in_dim(block, me * width, width, dim).astype(jnp.float32)
    for distance in range(1, count):
        route = [(i, (i + distance) % count) for i in range(count)]
        piece = lax.dynamic_slice_in_dim(block, ((me + distance) % count) * width, width, dim)
        total = total + lax.ppermute(piece, axis, route).astype(jnp.float32)
    return total


def shards(query_states, key_states, value_states, positions, out_weight, cotangent):
    local_tokens = query_states.shape[0]
    query_heads = split_heads(query_states)
    local_heads = query_heads.shape[1]
    model_cols = key_states.shape[1]
    packed = jnp.concatenate([key_states, value_states], axis=1)
    all_packed = lax.all_gather(packed, "seq", axis=0, tiled=True)
    all_keys = all_packed[:, :model_cols]
    all_values = all_packed[:, model_cols:]
    all_pos = lax.all_gather(positions, "seq", axis=0, tiled=True)
    key_heads = split_heads(all_keys)
    value_heads = split_heads(all_values)
    scores = masked_scores(query_heads, key_heads, positions, all_pos)
    row_max = jnp.max(scores, axis=2)
    log_total = row_max + jnp.log(jnp.sum(jnp.exp(scores - row_max[:, :, None]), axis=2))
    probs = jnp.exp(scores - log_total[:, :, None])
    weights = probs.astype(jnp.bfloat16)
    attended = jnp.einsum(
        "hqk,khd->qhd", weights, value_heads, preferred_element_type=jnp.float32
    )
    attended_heads = attended.astype(jnp.bfloat16)
    attended_flat = attended_heads.reshape(local_tokens, local_heads * HEAD_DIM)
    weight_full = lax.all_gather(out_weight, "seq", axis=1, tiled=True)
    partial_sum = jnp.dot(attended_flat, weight_full, preferred_element_type=jnp.float32).astype(
        jnp.bfloat16
    )
    cotangent_full = permute_gather(cotangent, "fsdp", 1)
    grad_attended = jnp.einsum(
        "td,hd->th", cotangent_full, weight_full, preferred_element_type=jnp.float32
    ).astype(jnp.bfloat16)
    partial_sum, grad_attended = lax.optimization_barrier((partial_sum, grad_attended))
    attn_output = permute_sum_scatter(partial_sum, "fsdp", 1)
    all_attended = lax.all_gather(attended_flat, "seq", axis=0, tiled=True)
    cotangent_cols = lax.all_to_all(cotangent_full, "seq", 1, 0, tiled=True)
    grad_heads = split_heads(grad_attended)
    row_delta = jnp.sum(
        grad_heads.astype(jnp.float32) * attended_heads.astype(jnp.float32), axis=2
    ).T
    halves = 2 if local_heads % 2 == 0 else 1
    span = local_heads // halves
    query_sums, key_sums, value_sums = [], [], []
    for half in range(halves):
        heads = slice(half * span, (half + 1) * span)
        half_grads = grad_heads[:, heads]
        grad_probs = jnp.einsum(
            "qhd,khd->hqk", half_grads, value_heads[:, heads], preferred_element_type=jnp.float32
        )
        grad_scores = (probs[heads] * (grad_probs - row_delta[heads, :, None])).astype(
            jnp.bfloat16
        )
        query_sums.append(
            jnp.einsum(
                "hqk,khd->qhd", grad_scores, key_heads[:, heads], preferred_element_type=jnp.float32
            )
        )
        key_part = jnp.einsum(
            "hqk,qhd->khd", grad_scores, query_heads[:, heads], preferred_element_type=jnp.float32
        )
        value_part = jnp.einsum(
            "hqk,qhd->khd", weights[heads], half_grads, preferred_element_type=jnp.float32
        )
        both_parts = jnp.concatenate([key_part, value_part], axis=1).astype(jnp.bfloat16)
        if half == 0:
            all_attended, both_parts = lax.optimization_barrier((all_attended, both_parts))
        both_sums = lax.psum_scatter(both_parts, "seq", scatter_dimension=0, tiled=True).astype(
            jnp.float32
        )
        key_sums.append(both_sums[:, :span])
        value_sums.append(both_sums[:, span:])
    grad_weight = jnp.einsum(
        "th,td->hd", all_attended, cotangent_cols, preferred_element_type=jnp.float32
    )
    query_sum = jnp.concatenate(query_sums, axis=1)
    key_sum = jnp.concatenate(key_sums, axis=1)
    value_sum = jnp.concatenate(value_sums, axis=1)
    score_scale = HEAD_DIM ** (-0.5)
    grad_queries = (query_sum * score_scale).reshape(local_tokens, local_heads * HEAD_DIM)
    grad_keys = (key_sum * score_scale).reshape(local_tokens, local_heads * HEAD_DIM)
    grad_values = value_sum.reshape(local_tokens, local_heads * HEAD_DIM)
    return (attn_output, grad_queries, grad_keys, grad_values, grad_weight)


def solution(mesh):
    in_specs = (
        P("seq", "fsdp"),
        P("seq", "fsdp"),
        P("seq", "fsdp"),
        P("seq"),
        P("fsdp", "seq"),
        P("seq", "fsdp"),
    )
    out_specs = (
        P("seq", "fsdp"),
        P("seq", "fsdp"),
        P("seq", "fsdp"),
        P("seq", "fsdp"),
        P("fsdp", "seq"),
    )
    return jax.shard_map(shards, mesh=mesh, in_specs=in_specs, out_specs=out_specs, check_vma=False)
```

```python
import jax
import jax.numpy as jnp
from jax import lax
from jax.sharding import PartitionSpec as P

HEAD_DIM = 128


blocked = -1e30


def split_heads(matrix):
    return matrix.reshape(matrix.shape[0], -1, HEAD_DIM)


def masked_scores(query_rows, key_rows, query_pos, key_pos):
    raw = jnp.einsum(
        "qhd,khd->hqk", query_rows, key_rows, preferred_element_type=jnp.float32
    ) * HEAD_DIM ** (-0.5)
    visible = key_pos[None, None, :] <= query_pos[None, :, None]
    return jnp.where(visible, raw, blocked)


def shift_pieces(block, axis):
    count = lax.axis_size(axis)
    pieces = [block]
    for distance in range(1, count):
        route = [(i, (i + distance) % count) for i in range(count)]
        pieces.append(lax.ppermute(block, axis, route))
    return pieces


def permute_gather(block, axis, dim):
    count = lax.axis_size(axis)
    me = lax.axis_index(axis)
    width = block.shape[dim]
    shape = list(block.shape)
    shape[dim] = width * count
    full = jnp.zeros(shape, block.dtype)
    for distance, piece in enumerate(shift_pieces(block, axis)):
        start = [0] * block.ndim
        start[dim] = ((me - distance) % count) * width
        full = lax.dynamic_update_slice(full, piece, start)
    return full


def permute_sum_scatter(block, axis, dim):
    count = lax.axis_size(axis)
    me = lax.axis_index(axis)
    width = block.shape[dim] // count
    total = lax.dynamic_slice_in_dim(block, me * width, width, dim).astype(jnp.float32)
    for distance in range(1, count):
        route = [(i, (i + distance) % count) for i in range(count)]
        piece = lax.dynamic_slice_in_dim(block, ((me + distance) % count) * width, width, dim)
        total = total + lax.ppermute(piece, axis, route).astype(jnp.float32)
    return total


def shards(query_states, key_states, value_states, positions, out_weight, cotangent):
    local_tokens = query_states.shape[0]
    query_heads = split_heads(query_states)
    local_heads = query_heads.shape[1]
    model_cols = key_states.shape[1]
    packed = jnp.concatenate([key_states, value_states], axis=1)
    all_packed = lax.all_gather(packed, "seq", axis=0, tiled=True)
    all_keys = all_packed[:, :model_cols]
    all_values = all_packed[:, model_cols:]
    all_pos = lax.all_gather(positions, "seq", axis=0, tiled=True)
    key_heads = split_heads(all_keys)
    value_heads = split_heads(all_values)
    scores = masked_scores(query_heads, key_heads, positions, all_pos)
    row_max = jnp.max(scores, axis=2)
    log_total = row_max + jnp.log(jnp.sum(jnp.exp(scores - row_max[:, :, None]), axis=2))
    probs = jnp.exp(scores - log_total[:, :, None])
    weights = probs.astype(jnp.bfloat16)
    attended = jnp.einsum(
        "hqk,khd->qhd", weights, value_heads, preferred_element_type=jnp.float32
    )
    attended_heads = attended.astype(jnp.bfloat16)
    attended_flat = attended_heads.reshape(local_tokens, local_heads * HEAD_DIM)
    weight_full = lax.all_gather(out_weight, "seq", axis=1, tiled=True)
    partial_sum = jnp.dot(attended_flat, weight_full, preferred_element_type=jnp.float32).astype(
        jnp.bfloat16
    )
    attn_output = permute_sum_scatter(partial_sum, "fsdp", 1)
    cotangent_full = permute_gather(cotangent, "fsdp", 1)
    grad_attended = jnp.einsum(
        "td,hd->th", cotangent_full, weight_full, preferred_element_type=jnp.float32
    ).astype(jnp.bfloat16)
    all_attended = lax.all_gather(attended_flat, "seq", axis=0, tiled=True)
    cotangent_cols = lax.all_to_all(cotangent_full, "seq", 1, 0, tiled=True)
    grad_weight = jnp.einsum(
        "th,td->hd", all_attended, cotangent_cols, preferred_element_type=jnp.float32
    )
    grad_heads = split_heads(grad_attended)
    row_delta = jnp.sum(
        grad_heads.astype(jnp.float32) * attended_heads.astype(jnp.float32), axis=2
    ).T
    grad_probs = jnp.einsum(
        "qhd,khd->hqk", grad_heads, value_heads, preferred_element_type=jnp.float32
    )
    grad_scores = (probs * (grad_probs - row_delta[:, :, None])).astype(jnp.bfloat16)
    query_sum = jnp.einsum(
        "hqk,khd->qhd", grad_scores, key_heads, preferred_element_type=jnp.float32
    )
    key_part = jnp.einsum(
        "hqk,qhd->khd", grad_scores, query_heads, preferred_element_type=jnp.float32
    )
    value_part = jnp.einsum(
        "hqk,qhd->khd", weights, grad_heads, preferred_element_type=jnp.float32
    )
    both_parts = jnp.concatenate([key_part, value_part], axis=1).astype(jnp.bfloat16)
    attn_output, both_parts = lax.optimization_barrier((attn_output, both_parts))
    both_sums = lax.psum_scatter(both_parts, "seq", scatter_dimension=0, tiled=True).astype(
        jnp.float32
    )
    key_sum = both_sums[:, :local_heads]
    value_sum = both_sums[:, local_heads:]
    score_scale = HEAD_DIM ** (-0.5)
    grad_queries = (query_sum * score_scale).reshape(local_tokens, local_heads * HEAD_DIM)
    grad_keys = (key_sum * score_scale).reshape(local_tokens, local_heads * HEAD_DIM)
    grad_values = value_sum.reshape(local_tokens, local_heads * HEAD_DIM)
    return (attn_output, grad_queries, grad_keys, grad_values, grad_weight)


def solution(mesh):
    in_specs = (
        P("seq", "fsdp"),
        P("seq", "fsdp"),
        P("seq", "fsdp"),
        P("seq"),
        P("fsdp", "seq"),
        P("seq", "fsdp"),
    )
    out_specs = (
        P("seq", "fsdp"),
        P("seq", "fsdp"),
        P("seq", "fsdp"),
        P("seq", "fsdp"),
        P("fsdp", "seq"),
    )
    return jax.shard_map(shards, mesh=mesh, in_specs=in_specs, out_specs=out_specs, check_vma=False)
```
